512 devices in a mesh: cfg: 2 (over x_lo), seq: 32 (over z, core), wgt: 8 (over y, x_hi).
Axes of the slice: x: 4 (x_hi: 2, x_lo: 2; x = x_hi * 2 + x_lo), y: 4, z: 16, core: 2. Of those that a mesh axis runs over, the one named last changes fastest.
Arguments:
- latent: float32 [1024, 4, 64], P(('seq', 'wgt'), 'cfg'), may hold values from -6 to 6
- img_hidden: bfloat16 [2, 1024, 4, 2432], P('cfg', 'seq'), may hold values from -5 to 5
- txt_hidden: bfloat16 [2, 512, 2432], P('cfg', 'seq'), may hold values from -6 to 6
- segments: int32 [2, 512], P('cfg', 'seq'), may hold values from 0 to 3, never falling along the last dimension, each value on 1 to 154 neighbouring positions
- timesteps: int32 [4], replicated, may hold values from 0 to 27
- modulation: float32 [2, 4, 10, 2432], P('cfg'), may hold values from -3 to 3
- qk_gain: float32 [2, 64], replicated, may hold values from 1.5 to 8
- qkv_weight: bfloat16 [3, 2432, 1536], P(None, 'seq', 'wgt'), may hold values from -0.08111071 to 0.08111071, as said below
- text_weight: bfloat16 [2, 2432, 1536], P(None, 'seq', 'wgt'), may hold values from -0.125 to 0.125
- out_weight: bfloat16 [1536, 2432], P('wgt', 'seq'), may hold values from -0.15625 to 0.15625
- expand_weight: bfloat16 [2432, 5632], P('seq', 'wgt'), may hold values from -0.125 to 0.125
- contract_weight: bfloat16 [5632, 2432], P('wgt', 'seq'), may hold values from -0.078125 to 0.078125
- final_weight: bfloat16 [2432, 64], replicated, may hold values from -0.0625 to 0.0625
Outputs:
- velocity: float32 [1024, 4, 64], P(('seq', 'wgt'), 'cfg')
- next_latent: float32 [1024, 4, 64], P(('seq', 'wgt'), 'cfg')
The draws below stay inside these ranges and needn't reach their ends.
Inputs may be any that keep to these rules, and one draw needn't show every extreme that they name: `segments`: along each row the segment never falls, and each request has 1 to 154 positions. `qkv_weight`: entries are of order 2432 ** -0.5.
All inputs are finite; a program needn't handle non-finite values.
Results may differ from the reference program's by a relative error of at most 0.012.
The reference program's roundings to bfloat16 on the way (of `image_normed`, `text_normed`, `attended`, `branch_in`, `expanded` and `final_in`) count: a program that leaves them out, or rounds other values in their place, can miss the bound.
Values may be sent and summed in bfloat16 or wider, within the bound.
No kernel may reach another device: no remote copies, remote signals or barrier semaphores. Data moves between devices by JAX's collectives and lax.ppermute only.
A program may use at most 128 MiB of HBM per device.

```python
import math
import jax
import jax.numpy as jnp
import numpy as np
from jax import lax

D = 2432
HEAD = 64
CH = 64
H = 24
FF = 5632
IMG = 1024
TXT_MOST = 154
STEPS = 28
R = 4
HD = 1536
TXT_ALL = 512
N_WGT = 8


def draw_img_hidden(key, part):
    values = jax.random.truncated_normal(key, -5.0, 5.0, (2, IMG, R, D), jnp.float32)
    return values.astype(jnp.bfloat16)


def draw_qk_gain(key, part):
    return jax.random.uniform(key, (2, HEAD), jnp.float32, 1.5, 2.5)


def draw_qkv_weight(key, part):
    values = jax.random.truncated_normal(key, -4.0, 4.0, (3, D, HD), jnp.float32) * D ** (-0.5)
    return values.astype(jnp.bfloat16)


def plant(array, rng, low, top_value):
    longest = array.shape.index(max(array.shape))
    spots = []
    for shift in (0, 1):
        where = [jax.random.randint(jax.random.fold_in(rng, axis), (), 0, length) for axis, length in enumerate(array.shape)]
        where[longest] = (where[longest] + shift) % array.shape[longest]
        spots.append(tuple(where))
    return array.at[spots[0]].set(low).at[spots[1]].set(top_value)


def block_levels(key, shape, pieces, least, top_value):
    def one(axis_at, blocks):
        draws = jax.random.uniform(jax.random.fold_in(jax.random.fold_in(key, 6), axis_at), (blocks,), jnp.float32, least / len(pieces), top_value / len(pieces))
        return jnp.repeat(jnp.exp(draws), shape[axis_at] // blocks).reshape((-1,) + (1,) * (len(shape) - axis_at - 1))

    loudness = one(*pieces[0])
    for cut in pieces[1:]:
        loudness = loudness * one(*cut)
    return loudness


def split_up(amount, total, limit, slope):
    loads = [(1 << 20) // math.isqrt(rank ** slope) + 1 for rank in range(2, amount + 1)]
    spare, counts = total - limit - (amount - 1), [1] * (amount - 1)
    while spare > 0:
        candidates = [i for i in range(amount - 1) if counts[i] < limit]
        whole, left = sum([loads[i] for i in candidates]), spare
        for i in candidates:
            addition = min(limit - counts[i], max(1, left * loads[i] // whole), spare)
            counts[i] = counts[i] + addition
            spare = spare - addition
    return np.array([limit] + counts)


def ragged(key, count, total, reach, skew):
    if count == 2:
        one = jax.random.randint(key, (), max(1, total - reach), min(reach, total - 1) + 1)
        return jnp.stack([one, total - one])
    lengths = jnp.asarray(split_up(count, total, reach, skew), jnp.int32)
    couples = (count - 1) // 2
    giver, taker = lengths[1:1 + 2 * couples:2], lengths[2:2 + 2 * couples:2]
    margin = jnp.minimum(giver - 1, reach - taker)
    passed = jax.random.randint(jax.random.fold_in(key, 1), (couples,), 0, 1 << 20) % (margin + 1)
    lengths = lengths.at[1:1 + 2 * couples:2].set(giver - passed).at[2:2 + 2 * couples:2].set(taker + passed)
    return lengths[jax.random.permutation(jax.random.fold_in(key, 2), count)]


def noise(own_key, extent, scale, reach, cuts=(), kind=jnp.bfloat16):
    factor_of = block_levels(own_key, extent, cuts, -0.22, 0.18) if cuts else 1.0
    values = jax.random.normal(own_key, extent, jnp.float32) * scale * factor_of
    return jnp.minimum(jnp.maximum(values, -reach), reach).astype(kind)


def setup_inputs(seed: int = 0) -> dict:
    key_of = jax.random.split(jax.random.key(seed), 14)
    latent = noise(key_of[0], (IMG, R, CH), 1.0, 6.0, ((0, 256), (1, 2)), jnp.float32)
    img_hidden = draw_img_hidden(jax.random.fold_in(key_of[13], 71), 0)
    txt_hidden = noise(key_of[2], (2, TXT_ALL, D), 1.0, 6.0, ((0, 2), (1, 32)))
    segments = jax.vmap(lambda own: jnp.searchsorted(jnp.cumsum(ragged(own, R, TXT_ALL, TXT_MOST, 1)), jnp.arange(TXT_ALL), side="right"))(jax.random.split(key_of[3], 2)).reshape((2, TXT_ALL)).astype(jnp.int32)
    timesteps = plant(jax.random.randint(key_of[4], (R,), 0, STEPS), jax.random.fold_in(key_of[4], 1), 0, STEPS - 1).astype(jnp.int32)
    modulation = noise(key_of[5], (2, R, 10, D), 0.5, 3.0, ((0, 2),), jnp.float32)
    qk_gain = draw_qk_gain(jax.random.fold_in(key_of[13], 71), 0)
    qkv_weight = draw_qkv_weight(jax.random.fold_in(key_of[13], 71), 0)
    text_weight = noise(key_of[8], (2, D, HD), D ** -0.5, 0.125, ((1, 32), (2, 8)))
    out_weight = noise(key_of[9], (HD, D), HD ** -0.5, 0.15625, ((0, 8), (1, 32)))
    expand_weight = noise(key_of[10], (D, FF), D ** -0.5, 0.125, ((0, 32), (1, 8)))
    contract_weight = noise(key_of[11], (FF, D), FF ** -0.5, 0.078125, ((0, 8), (1, 32)))
    final_weight = noise(key_of[12], (D, CH), (4 * D) ** -0.5, 0.0625)
    return {"latent": latent, "img_hidden": img_hidden, "txt_hidden": txt_hidden, "segments": segments, "timesteps": timesteps, "modulation": modulation, "qk_gain": qk_gain, "qkv_weight": qkv_weight, "text_weight": text_weight, "out_weight": out_weight, "expand_weight": expand_weight, "contract_weight": contract_weight, "final_weight": final_weight}


guidance_scale = 3.5
flow_shift = 3.0
eps_norm = 1e-06
masked_score = -1e+30

def layer_norm(values):
    center = lax.optimization_barrier(jnp.mean(values, axis=-1, keepdims=True))
    centred = values - center
    spread = lax.optimization_barrier(jnp.mean(centred * centred, axis=-1, keepdims=True))
    return centred * lax.rsqrt(spread + eps_norm)

def head_norm(values, gain_row):
    power = lax.optimization_barrier(jnp.mean(values * values, axis=-1, keepdims=True))
    return values * lax.rsqrt(power + eps_norm) * gain_row

def sigma_of(index_row):
    time_left = 1.0 - index_row.astype(jnp.float32) / STEPS
    return flow_shift * time_left / (1.0 + (flow_shift - 1.0) * time_left)

def rounded(values):
    return lax.optimization_barrier(values.astype(jnp.bfloat16)).astype(jnp.float32)

def half_velocity(hidden, text_rows, segment_row, modulate, qk_gain, qkv_weight, text_weight, out_weight, expand_weight, contract_weight, final_weight):
    hidden_f = hidden.astype(jnp.float32)
    image_normed = (layer_norm(hidden_f) * (1.0 + modulate[:, 1]) + modulate[:, 0]).astype(jnp.bfloat16)
    one_hot = (segment_row[:, None] == jnp.arange(R, dtype=jnp.int32)[None, :]).astype(jnp.float32)
    text_mod = jnp.einsum('tr,rkd->tkd', one_hot, modulate[:, 3:5], precision=lax.Precision.HIGHEST)
    text_normed = (layer_norm(text_rows.astype(jnp.float32)) * (1.0 + text_mod[:, 1]) + text_mod[:, 0]).astype(jnp.bfloat16)
    flat_rows = image_normed.reshape(IMG * R, D)
    queries = jnp.dot(flat_rows, qkv_weight[0], preferred_element_type=jnp.float32).reshape(IMG, R, H, HEAD)
    keys_img = jnp.dot(flat_rows, qkv_weight[1], preferred_element_type=jnp.float32).reshape(IMG, R, H, HEAD)
    values_img = jnp.dot(flat_rows, qkv_weight[2], preferred_element_type=jnp.float32).reshape(IMG, R, H, HEAD)
    queries = rounded(head_norm(queries, qk_gain[0]))
    keys_img = rounded(head_norm(keys_img, qk_gain[1]))
    values_img = rounded(values_img)
    keys_txt = jnp.dot(text_normed, text_weight[0], preferred_element_type=jnp.float32).reshape(TXT_ALL, H, HEAD)
    keys_txt = rounded(head_norm(keys_txt, qk_gain[1]))
    values_txt = rounded(jnp.dot(text_normed, text_weight[1], preferred_element_type=jnp.float32).reshape(TXT_ALL, H, HEAD))
    scale_factor = HEAD ** (-0.5)

    def attend(request):
        query_r = lax.dynamic_index_in_dim(queries, request, 1, keepdims=False)
        key_r = lax.dynamic_index_in_dim(keys_img, request, 1, keepdims=False)
        value_r = lax.dynamic_index_in_dim(values_img, request, 1, keepdims=False)
        image_scores = jnp.einsum('qhd,khd->hqk', query_r, key_r) * scale_factor
        text_scores = jnp.einsum('qhd,khd->hqk', query_r, keys_txt) * scale_factor
        allowed = segment_row == request
        text_scores = jnp.where(allowed[None, None, :], text_scores, masked_score)
        scores = jnp.concatenate([image_scores, text_scores], axis=2)
        row_max = lax.optimization_barrier(jnp.max(scores, axis=2, keepdims=True))
        weights = jnp.exp(scores - row_max)
        row_sum = lax.optimization_barrier(jnp.sum(weights, axis=2, keepdims=True))
        all_values = jnp.concatenate([value_r, values_txt], axis=0)
        mixed_heads = jnp.einsum('hqk,khd->hqd', rounded(weights), all_values) / row_sum
        return jnp.transpose(mixed_heads, (1, 0, 2)).astype(jnp.bfloat16)
    attended = lax.map(attend, jnp.arange(R, dtype=jnp.int32))
    attended = jnp.transpose(attended, (1, 0, 2, 3)).reshape(IMG * R, HD)
    group_cols = HD // N_WGT
    mixed = jnp.zeros((IMG * R, D), jnp.float32)
    for group in range(N_WGT):
        term = jnp.dot(attended[:, group * group_cols:(group + 1) * group_cols], out_weight[group * group_cols:(group + 1) * group_cols], preferred_element_type=jnp.float32)
        mixed = mixed + rounded(term)
    residual = hidden_f + modulate[:, 2] * mixed.reshape(IMG, R, D)
    branch_in = (layer_norm(residual) * (1.0 + modulate[:, 6]) + modulate[:, 5]).astype(jnp.bfloat16)
    expanded = jnp.dot(branch_in.reshape(IMG * R, D), expand_weight, preferred_element_type=jnp.float32)
    expanded = jax.nn.gelu(expanded, approximate=True).astype(jnp.bfloat16)
    unit_cols = FF // N_WGT
    branch = jnp.zeros((IMG * R, D), jnp.float32)
    for group in range(N_WGT):
        term = jnp.dot(expanded[:, group * unit_cols:(group + 1) * unit_cols], contract_weight[group * unit_cols:(group + 1) * unit_cols], preferred_element_type=jnp.float32)
        branch = branch + rounded(term)
    second = residual + modulate[:, 7] * branch.reshape(IMG, R, D)
    final_in = (layer_norm(second) * (1.0 + modulate[:, 9]) + modulate[:, 8]).astype(jnp.bfloat16)
    return jnp.dot(final_in.reshape(IMG * R, D), final_weight, preferred_element_type=jnp.float32).reshape(IMG, R, CH)

def reference(latent, img_hidden, txt_hidden, segments, timesteps, modulation, qk_gain, qkv_weight, text_weight, out_weight, expand_weight, contract_weight, final_weight):
    results = []
    for half_index in range(2):
        results.append(half_velocity(img_hidden[half_index], txt_hidden[half_index], segments[half_index], modulation[half_index], qk_gain, qkv_weight, text_weight, out_weight, expand_weight, contract_weight, final_weight))
    velocity = results[1] + guidance_scale * (results[0] - results[1])
    step_size = sigma_of(timesteps + 1) - sigma_of(timesteps)
    next_latent = latent + step_size[None, :, None] * velocity
    return (velocity, next_latent)
```

```python
import jax
import jax.numpy as jnp
from jax import lax
from jax.sharding import PartitionSpec as P

STEPS = 28


guidance_scale = 3.5
flow_shift = 3.0
eps_norm = 1e-06
masked_score = -1e30


def from_partner(value, axis, bit):
    mask = 2**bit
    pairs = [(source, source ^ mask) for source in range(lax.axis_size(axis))]
    return lax.ppermute(value, axis, pairs)


def layer_norm(values):
    center = jnp.mean(values, axis=-1, keepdims=True)
    centred = values - center
    spread = jnp.mean(centred * centred, axis=-1, keepdims=True)
    return centred * lax.rsqrt(spread + eps_norm)


def head_norm(values, gain_row):
    power = jnp.mean(values * values, axis=-1, keepdims=True)
    return values * lax.rsqrt(power + eps_norm) * gain_row


def sigma_of(index_row):
    time_left = 1.0 - index_row.astype(jnp.float32) / STEPS
    return flow_shift * time_left / (1.0 + (flow_shift - 1.0) * time_left)


def group_sum(partial, groups):
    swapped = lax.all_to_all(partial, "wgt", 0, 0, tiled=True)
    rows = swapped.shape[0] // groups
    return jnp.sum(swapped.reshape(groups, rows, -1).astype(jnp.float32), axis=0)


def body(
    latent,
    img_hidden,
    txt_hidden,
    segments,
    timesteps,
    modulation,
    qk_gain,
    qkv_weight,
    text_weight,
    out_weight,
    expand_weight,
    contract_weight,
    final_weight,
):
    tokens_here = img_hidden.shape[1]
    requests = img_hidden.shape[2]
    feat_width = img_hidden.shape[3]
    head_size = qk_gain.shape[1]
    local_cols = qkv_weight.shape[2]
    heads_here = local_cols // head_size
    text_here = txt_hidden.shape[1]
    seq_size = lax.axis_size("seq")
    wgt_size = lax.axis_size("wgt")
    modulate = modulation[0]
    hidden = img_hidden[0].astype(jnp.float32)
    image_normed = (layer_norm(hidden) * (1.0 + modulate[:, 1]) + modulate[:, 0]).astype(
        jnp.bfloat16
    )
    row_count = tokens_here * requests
    token_rows = image_normed.reshape(row_count, feat_width)
    segment_row = segments[0]
    one_hot = (segment_row[:, None] == jnp.arange(requests, dtype=jnp.int32)[None, :]).astype(
        jnp.float32
    )
    text_mod = jnp.einsum("tr,rkd->tkd", one_hot, modulate[:, 3:5], precision=lax.Precision.HIGHEST)
    text_normed = (
        layer_norm(txt_hidden[0].astype(jnp.float32)) * (1.0 + text_mod[:, 1]) + text_mod[:, 0]
    ).astype(jnp.bfloat16)
    all_weights = jnp.concatenate([qkv_weight, text_weight], axis=0)
    piece = lax.all_gather(all_weights, "seq", axis=1, tiled=True)
    mlp_local = jnp.stack([expand_weight, contract_weight.T], axis=0)
    mlp_full = lax.all_gather(mlp_local, "seq", axis=1, tiled=True)
    out_full = lax.all_gather(out_weight, "seq", axis=1, tiled=True)
    both_rows = jnp.concatenate([token_rows, text_normed], axis=0)
    both_term = jnp.einsum(
        "rd,kdc->rkc", both_rows, piece, preferred_element_type=jnp.float32
    )
    image_term = both_term[:row_count]
    text_term = both_term[row_count:]
    queries = head_norm(
        image_term[:, 0].reshape(tokens_here, requests, heads_here, head_size), qk_gain[0]
    ).astype(jnp.bfloat16)
    keys_img = head_norm(
        image_term[:, 1].reshape(tokens_here, requests, heads_here, head_size), qk_gain[1]
    ).astype(jnp.bfloat16)
    values_img = image_term[:, 2].reshape(tokens_here, requests, local_cols).astype(jnp.bfloat16)
    keys_txt = head_norm(
        text_term[:, 3].reshape(text_here, heads_here, head_size), qk_gain[1]
    ).astype(jnp.bfloat16)
    values_txt = text_term[:, 4].astype(jnp.bfloat16)
    image_pair = jnp.stack(
        [keys_img.reshape(tokens_here, requests, local_cols), values_img], axis=2
    ).reshape(tokens_here * requests * 2, local_cols)
    text_pair = jnp.stack([keys_txt.reshape(text_here, local_cols), values_txt], axis=1).reshape(
        text_here * 2, local_cols
    )
    owner_row = jnp.pad(
        segment_row.astype(jnp.float32).astype(jnp.bfloat16), (0, local_cols - text_here)
    )[None, :]
    image_len = tokens_here * requests * 2
    shared = jnp.concatenate([image_pair, text_pair, owner_row], axis=0)
    shared_piece = lax.all_gather(shared, "seq", axis=0, tiled=False)
    image_piece = shared_piece[:, :image_len].reshape(
        seq_size * tokens_here, requests, 2, local_cols
    )
    text_piece = shared_piece[:, image_len : image_len + 2 * text_here].reshape(
        seq_size * text_here, 2, local_cols
    )
    owner_piece = shared_piece[:, image_len + 2 * text_here, :text_here].reshape(-1)
    scale_factor = head_size ** (-0.5)
    request_ids = jnp.arange(requests, dtype=jnp.float32)
    piece_keys = image_piece[:, :, 0].reshape(-1, requests, heads_here, head_size)
    piece_values = image_piece[:, :, 1].reshape(-1, requests, heads_here, head_size)
    text_keys = text_piece[:, 0].reshape(-1, heads_here, head_size)
    text_values = text_piece[:, 1].reshape(-1, heads_here, head_size)
    image_scores = (
        jnp.einsum("qrhd,krhd->rhqk", queries, piece_keys, preferred_element_type=jnp.float32)
        * scale_factor
    )
    text_scores = (
        jnp.einsum("qrhd,khd->rhqk", queries, text_keys, preferred_element_type=jnp.float32)
        * scale_factor
    )
    allowed = owner_piece.astype(jnp.float32)[None, :] == request_ids[:, None]
    text_scores = jnp.where(allowed[:, None, None, :], text_scores, masked_score)
    row_max = jnp.maximum(jnp.max(image_scores, axis=-1), jnp.max(text_scores, axis=-1))
    image_weights = jnp.exp(image_scores - row_max[..., None])
    text_weights = jnp.exp(text_scores - row_max[..., None])
    row_sum = jnp.sum(image_weights, axis=-1) + jnp.sum(text_weights, axis=-1)
    acc = jnp.einsum(
        "rhqk,krhd->rhqd",
        image_weights.astype(jnp.bfloat16),
        piece_values,
        preferred_element_type=jnp.float32,
    )
    acc = acc + jnp.einsum(
        "rhqk,khd->rhqd",
        text_weights.astype(jnp.bfloat16),
        text_values,
        preferred_element_type=jnp.float32,
    )
    attended = acc / row_sum[..., None]
    attended = (
        jnp.transpose(attended, (2, 0, 1, 3)).reshape(row_count, local_cols).astype(jnp.bfloat16)
    )
    share_rows = row_count // wgt_size
    mixed = group_sum(
        jnp.dot(attended, out_full, preferred_element_type=jnp.float32).astype(jnp.bfloat16),
        wgt_size,
    )
    tokens_out = share_rows // requests
    row_place = lax.axis_index("wgt") * share_rows
    base_rows = lax.dynamic_slice_in_dim(
        hidden.reshape(row_count, feat_width), row_place, share_rows, 0
    )
    residual = base_rows.reshape(tokens_out, requests, feat_width) + modulate[:, 2] * mixed.reshape(
        tokens_out, requests, feat_width
    )
    branch_in = (layer_norm(residual) * (1.0 + modulate[:, 6]) + modulate[:, 5]).astype(
        jnp.bfloat16
    )
    branch_rows = lax.all_gather(
        branch_in.reshape(share_rows, feat_width), "wgt", axis=0, tiled=True
    )
    expanded = jnp.dot(branch_rows, mlp_full[0], preferred_element_type=jnp.float32)
    expanded = jax.nn.gelu(expanded, approximate=True).astype(jnp.bfloat16)
    branch = group_sum(
        jnp.einsum(
            "rf,df->rd", expanded, mlp_full[1], preferred_element_type=jnp.float32
        ).astype(jnp.bfloat16),
        wgt_size,
    )
    second = residual + modulate[:, 7] * branch.reshape(tokens_out, requests, feat_width)
    final_in = (layer_norm(second) * (1.0 + modulate[:, 9]) + modulate[:, 8]).astype(jnp.bfloat16)
    own_velocity = jnp.dot(
        final_in.reshape(share_rows, feat_width), final_weight, preferred_element_type=jnp.float32
    ).reshape(tokens_out, requests, -1)
    guide_side = lax.axis_index("cfg")
    guided_count = latent.shape[1]
    kept_rows = lax.dynamic_slice_in_dim(own_velocity, guide_side * guided_count, guided_count, 1)
    sent_rows = lax.dynamic_slice_in_dim(
        own_velocity, (1 - guide_side) * guided_count, guided_count, 1
    )
    partner_velocity = from_partner(sent_rows, "cfg", 0)
    is_first = guide_side == 0
    conditional = jnp.where(is_first, kept_rows, partner_velocity)
    unconditional = jnp.where(is_first, partner_velocity, kept_rows)
    velocity = unconditional + guidance_scale * (conditional - unconditional)
    step_size = sigma_of(timesteps + 1) - sigma_of(timesteps)
    step_here = lax.dynamic_slice_in_dim(step_size, guide_side * guided_count, guided_count, 0)
    next_latent = latent + step_here[None, :, None] * velocity
    return (velocity, next_latent)


def solution(mesh):
    return jax.shard_map(
        body,
        mesh=mesh,
        in_specs=(
            P(("seq", "wgt"), "cfg", None),
            P("cfg", "seq", None, None),
            P("cfg", "seq", None),
            P("cfg", "seq"),
            P(),
            P("cfg", None, None, None),
            P(),
            P(None, "seq", "wgt"),
            P(None, "seq", "wgt"),
            P("wgt", "seq"),
            P("seq", "wgt"),
            P("wgt", "seq"),
            P(),
        ),
        out_specs=(P(("seq", "wgt"), "cfg", None), P(("seq", "wgt"), "cfg", None)),
        check_vma=False,
    )
```

```python
import jax
import jax.numpy as jnp
from jax import lax
from jax.experimental import pallas as pl
from jax.experimental.pallas import tpu as pltpu
from jax.sharding import PartitionSpec as P

STEPS = 28


guidance_scale = 3.5
flow_shift = 3.0
eps_norm = 1e-06
masked_score = -1e30


def from_partner(value, axis, bit):
    mask = 2**bit
    pairs = [(source, source ^ mask) for source in range(lax.axis_size(axis))]
    return lax.ppermute(value, axis, pairs)


def layer_norm(values):
    center = jnp.mean(values, axis=-1, keepdims=True)
    centred = values - center
    spread = jnp.mean(centred * centred, axis=-1, keepdims=True)
    return centred * lax.rsqrt(spread + eps_norm)


def head_norm(values, gain_row):
    power = jnp.mean(values * values, axis=-1, keepdims=True)
    return values * lax.rsqrt(power + eps_norm) * gain_row


def sigma_of(index_row):
    time_left = 1.0 - index_row.astype(jnp.float32) / STEPS
    return flow_shift * time_left / (1.0 + (flow_shift - 1.0) * time_left)


def group_sum(partial, groups):
    swapped = lax.all_to_all(partial, "wgt", 0, 0, tiled=True)
    rows = swapped.shape[0] // groups
    return jnp.sum(swapped.reshape(groups, rows, -1).astype(jnp.float32), axis=0)


def make_attention(heads, head_size, text_at, text_here):
    scale = head_size ** (-0.5)

    def kernel(q_ref, kv_ref, mask_ref, o_ref):
        requests, tokens, cols = q_ref.shape
        blocks = kv_ref.shape[0]
        lane = lax.broadcasted_iota(jnp.int32, (1, cols), 1)
        k_txt = kv_ref[:, text_at : text_at + text_here, :].reshape(blocks * text_here, cols)
        v_txt = kv_ref[:, text_at + text_here : text_at + 2 * text_here, :].reshape(
            blocks * text_here, cols
        )
        dims = (((1,), (1,)), ((), ()))
        for r in range(requests):
            q = q_ref[r].astype(jnp.float32)
            k_img = kv_ref[:, 2 * tokens * r : 2 * tokens * r + tokens, :].reshape(
                blocks * tokens, cols
            )
            v_img = kv_ref[:, 2 * tokens * r + tokens : 2 * tokens * (r + 1), :].reshape(
                blocks * tokens, cols
            )
            allowed = mask_ref[r : r + 1, :] > 0.5
            out = jnp.zeros((tokens, cols), jnp.float32)
            for h in range(heads):
                in_head = (lane >= h * head_size) & (lane < (h + 1) * head_size)
                qh = jnp.where(in_head, q, 0.0).astype(jnp.bfloat16)
                s_img = lax.dot_general(qh, k_img, dims, preferred_element_type=jnp.float32) * scale
                s_txt = lax.dot_general(qh, k_txt, dims, preferred_element_type=jnp.float32) * scale
                s_txt = jnp.where(allowed, s_txt, masked_score)
                top = jnp.maximum(
                    jnp.max(s_img, axis=1, keepdims=True), jnp.max(s_txt, axis=1, keepdims=True)
                )
                p_img = jnp.exp(s_img - top)
                p_txt = jnp.exp(s_txt - top)
                total = jnp.sum(p_img, axis=1, keepdims=True) + jnp.sum(p_txt, axis=1, keepdims=True)
                acc = jnp.dot(
                    p_img.astype(jnp.bfloat16), v_img, preferred_element_type=jnp.float32
                ) + jnp.dot(p_txt.astype(jnp.bfloat16), v_txt, preferred_element_type=jnp.float32)
                out = jnp.where(in_head, acc / total, out)
            o_ref[r] = out.astype(o_ref.dtype)

    def run(q, kv, mask):
        return pl.pallas_call(
            kernel,
            out_shape=jax.ShapeDtypeStruct(q.shape, jnp.bfloat16),
            in_specs=[pl.BlockSpec(memory_space=pltpu.VMEM)] * 3,
            out_specs=pl.BlockSpec(memory_space=pltpu.VMEM),
        )(q, kv, mask)

    return run


def body(
    latent,
    img_hidden,
    txt_hidden,
    segments,
    timesteps,
    modulation,
    qk_gain,
    qkv_weight,
    text_weight,
    out_weight,
    expand_weight,
    contract_weight,
    final_weight,
):
    tokens_here = img_hidden.shape[1]
    requests = img_hidden.shape[2]
    feat_width = img_hidden.shape[3]
    head_size = qk_gain.shape[1]
    local_cols = qkv_weight.shape[2]
    heads_here = local_cols // head_size
    text_here = txt_hidden.shape[1]
    seq_size = lax.axis_size("seq")
    wgt_size = lax.axis_size("wgt")
    modulate = modulation[0]
    hidden = img_hidden[0].astype(jnp.float32)
    image_normed = (layer_norm(hidden) * (1.0 + modulate[:, 1]) + modulate[:, 0]).astype(
        jnp.bfloat16
    )
    row_count = tokens_here * requests
    token_rows = image_normed.reshape(row_count, feat_width)
    segment_row = segments[0]
    one_hot = (segment_row[:, None] == jnp.arange(requests, dtype=jnp.int32)[None, :]).astype(
        jnp.float32
    )
    text_mod = jnp.einsum("tr,rkd->tkd", one_hot, modulate[:, 3:5], precision=lax.Precision.HIGHEST)
    text_normed = (
        layer_norm(txt_hidden[0].astype(jnp.float32)) * (1.0 + text_mod[:, 1]) + text_mod[:, 0]
    ).astype(jnp.bfloat16)
    all_weights = jnp.concatenate([qkv_weight, text_weight], axis=0)
    piece = lax.all_gather(all_weights, "seq", axis=1, tiled=True)
    block_rows = expand_weight.shape[0]
    padded_rows = block_rows + (-block_rows) % 8
    mlp_local = jnp.pad(
        jnp.stack([expand_weight, contract_weight.T], axis=0),
        ((0, 0), (0, padded_rows - block_rows), (0, 0)),
    )
    mlp_full = lax.all_gather(mlp_local, "seq", axis=0, tiled=False)
    out_full = lax.all_gather(out_weight, "seq", axis=1, tiled=True)
    both_rows = jnp.concatenate([token_rows, text_normed], axis=0)
    both_term = jnp.einsum(
        "rd,kdc->rkc", both_rows, piece, preferred_element_type=jnp.float32
    )
    image_term = both_term[:row_count]
    text_term = both_term[row_count:]
    queries = head_norm(
        image_term[:, 0].reshape(tokens_here, requests, heads_here, head_size), qk_gain[0]
    ).astype(jnp.bfloat16)
    keys_img = head_norm(
        image_term[:, 1].reshape(tokens_here, requests, heads_here, head_size), qk_gain[1]
    ).astype(jnp.bfloat16)
    values_img = image_term[:, 2].reshape(tokens_here, requests, local_cols).astype(jnp.bfloat16)
    keys_txt = head_norm(
        text_term[:, 3].reshape(text_here, heads_here, head_size), qk_gain[1]
    ).astype(jnp.bfloat16)
    values_txt = text_term[:, 4].astype(jnp.bfloat16)
    image_pair = jnp.transpose(
        jnp.stack([keys_img.reshape(tokens_here, requests, local_cols), values_img], axis=0),
        (2, 0, 1, 3),
    ).reshape(requests * 2 * tokens_here, local_cols)
    text_pair = jnp.stack([keys_txt.reshape(text_here, local_cols), values_txt], axis=0).reshape(
        2 * text_here, local_cols
    )
    lanes = local_cols + (-local_cols) % 128
    image_pair = jnp.pad(image_pair, ((0, 0), (0, lanes - local_cols)))
    text_pair = jnp.pad(text_pair, ((0, 0), (0, lanes - local_cols)))
    owner_row = jnp.pad(
        segment_row.astype(jnp.float32).astype(jnp.bfloat16), (0, lanes - text_here)
    )[None, :]
    image_len = requests * 2 * tokens_here
    owner_at = image_len + 2 * text_here
    pad_rows = (-(owner_at + 1)) % 16
    shared = jnp.concatenate(
        [image_pair, text_pair, owner_row, jnp.zeros((pad_rows, lanes), jnp.bfloat16)], axis=0
    )
    shared_piece = lax.all_gather(shared, "seq", axis=0, tiled=False)
    owner_piece = shared_piece[:, owner_at, :text_here].reshape(-1)
    request_ids = jnp.arange(requests, dtype=jnp.float32)
    text_mask = (owner_piece.astype(jnp.float32)[None, :] == request_ids[:, None]).astype(
        jnp.float32
    )
    query_block = jnp.pad(
        jnp.transpose(queries.reshape(tokens_here, requests, local_cols), (1, 0, 2)),
        ((0, 0), (0, 0), (0, lanes - local_cols)),
    )
    attend = make_attention(heads_here, head_size, image_len, text_here)
    attended = attend(query_block, shared_piece, text_mask)
    attended = jnp.transpose(attended[:, :, :local_cols], (1, 0, 2)).reshape(row_count, local_cols)
    share_rows = row_count // wgt_size
    mixed = group_sum(
        jnp.dot(attended, out_full, preferred_element_type=jnp.float32).astype(jnp.bfloat16),
        wgt_size,
    )
    tokens_out = share_rows // requests
    row_place = lax.axis_index("wgt") * share_rows
    base_rows = lax.dynamic_slice_in_dim(
        hidden.reshape(row_count, feat_width), row_place, share_rows, 0
    )
    residual = base_rows.reshape(tokens_out, requests, feat_width) + modulate[:, 2] * mixed.reshape(
        tokens_out, requests, feat_width
    )
    branch_in = (layer_norm(residual) * (1.0 + modulate[:, 6]) + modulate[:, 5]).astype(
        jnp.bfloat16
    )
    branch_rows = lax.all_to_all(
        jnp.broadcast_to(
            branch_in.reshape(1, share_rows, feat_width), (wgt_size, share_rows, feat_width)
        ),
        "wgt",
        0,
        0,
        tiled=True,
    ).reshape(row_count, feat_width)
    padded_rows_in = jnp.pad(
        branch_rows.reshape(row_count, seq_size, block_rows),
        ((0, 0), (0, 0), (0, padded_rows - block_rows)),
    )
    expanded = jnp.einsum(
        "rsd,sdf->rf", padded_rows_in, mlp_full[:, 0], preferred_element_type=jnp.float32
    )
    expanded = jax.nn.gelu(expanded, approximate=True).astype(jnp.bfloat16)
    contracted = jnp.einsum(
        "rf,sdf->rsd", expanded, mlp_full[:, 1], preferred_element_type=jnp.float32
    )[:, :, :block_rows].reshape(row_count, feat_width)
    branch = group_sum(contracted.astype(jnp.bfloat16), wgt_size)
    second = residual + modulate[:, 7] * branch.reshape(tokens_out, requests, feat_width)
    final_in = (layer_norm(second) * (1.0 + modulate[:, 9]) + modulate[:, 8]).astype(jnp.bfloat16)
    own_velocity = jnp.dot(
        final_in.reshape(share_rows, feat_width), final_weight, preferred_element_type=jnp.float32
    ).reshape(tokens_out, requests, -1)
    guide_side = lax.axis_index("cfg")
    guided_count = latent.shape[1]
    kept_rows = lax.dynamic_slice_in_dim(own_velocity, guide_side * guided_count, guided_count, 1)
    sent_rows = lax.dynamic_slice_in_dim(
        own_velocity, (1 - guide_side) * guided_count, guided_count, 1
    )
    partner_velocity = from_partner(sent_rows, "cfg", 0)
    is_first = guide_side == 0
    conditional = jnp.where(is_first, kept_rows, partner_velocity)
    unconditional = jnp.where(is_first, partner_velocity, kept_rows)
    velocity = unconditional + guidance_scale * (conditional - unconditional)
    step_size = sigma_of(timesteps + 1) - sigma_of(timesteps)
    step_here = lax.dynamic_slice_in_dim(step_size, guide_side * guided_count, guided_count, 0)
    next_latent = latent + step_here[None, :, None] * velocity
    return (velocity, next_latent)


def solution(mesh):
    return jax.shard_map(
        body,
        mesh=mesh,
        in_specs=(
            P(("seq", "wgt"), "cfg", None),
            P("cfg", "seq", None, None),
            P("cfg", "seq", None),
            P("cfg", "seq"),
            P(),
            P("cfg", None, None, None),
            P(),
            P(None, "seq", "wgt"),
            P(None, "seq", "wgt"),
            P("wgt", "seq"),
            P("seq", "wgt"),
            P("wgt", "seq"),
            P(),
        ),
        out_specs=(P(("seq", "wgt"), "cfg", None), P(("seq", "wgt"), "cfg", None)),
        check_vma=False,
    )
```

```python
import jax
import jax.numpy as jnp
from jax import lax
from jax.experimental import pallas as pl
from jax.experimental.pallas import tpu as pltpu
from jax.sharding import Mesh, PartitionSpec as P

STEPS = 28


guidance_scale = 3.5
flow_shift = 3.0
eps_norm = 1e-06
masked_score = -1e30


def from_partner(value, axis, bit):
    mask = 2**bit
    pairs = [(source, source ^ mask) for source in range(lax.axis_size(axis))]
    return lax.ppermute(value, axis, pairs)


def layer_norm(values):
    center = jnp.mean(values, axis=-1, keepdims=True)
    centred = values - center
    spread = jnp.mean(centred * centred, axis=-1, keepdims=True)
    return centred * lax.rsqrt(spread + eps_norm)


def head_norm(values, gain_row):
    power = jnp.mean(values * values, axis=-1, keepdims=True)
    return values * lax.rsqrt(power + eps_norm) * gain_row


def sigma_of(index_row):
    time_left = 1.0 - index_row.astype(jnp.float32) / STEPS
    return flow_shift * time_left / (1.0 + (flow_shift - 1.0) * time_left)


SEQ = ("z", "core")


def chip_pair(block):
    other = from_partner(block, "core", 0)
    first = lax.axis_index("core") == 0
    return jnp.where(first, jnp.stack([block, other]), jnp.stack([other, block]))


def half_gather(block, axis):
    pair = chip_pair(block)
    width = pair.shape[axis + 1] // 2
    mine = lax.dynamic_slice_in_dim(pair, lax.axis_index("core") * width, width, axis + 1)
    gathered = lax.all_gather(mine, "z", axis=0, tiled=False)
    return gathered, from_partner(gathered, "core", 0)


def group_sum(partial, groups):
    swapped = lax.all_to_all(partial, "wgt", 0, 0, tiled=True)
    rows = swapped.shape[0] // groups
    return jnp.sum(swapped.reshape(groups, rows, -1).astype(jnp.float32), axis=0)


def make_attention(heads, head_size, text_at, text_here):
    scale = head_size ** (-0.5)

    def kernel(q_ref, kv_ref, mask_ref, o_ref):
        requests, tokens, cols = q_ref.shape
        blocks = kv_ref.shape[0]
        lane = lax.broadcasted_iota(jnp.int32, (1, cols), 1)
        k_txt = kv_ref[:, text_at : text_at + text_here, :].reshape(blocks * text_here, cols)
        v_txt = kv_ref[:, text_at + text_here : text_at + 2 * text_here, :].reshape(
            blocks * text_here, cols
        )
        dims = (((1,), (1,)), ((), ()))
        for r in range(requests):
            q = q_ref[r].astype(jnp.float32)
            k_img = kv_ref[:, 2 * tokens * r : 2 * tokens * r + tokens, :].reshape(
                blocks * tokens, cols
            )
            v_img = kv_ref[:, 2 * tokens * r + tokens : 2 * tokens * (r + 1), :].reshape(
                blocks * tokens, cols
            )
            allowed = mask_ref[r : r + 1, :] > 0.5
            out = jnp.zeros((tokens, cols), jnp.float32)
            for h in range(heads):
                in_head = (lane >= h * head_size) & (lane < (h + 1) * head_size)
                qh = jnp.where(in_head, q, 0.0).astype(jnp.bfloat16)
                s_img = lax.dot_general(qh, k_img, dims, preferred_element_type=jnp.float32) * scale
                s_txt = lax.dot_general(qh, k_txt, dims, preferred_element_type=jnp.float32) * scale
                s_txt = jnp.where(allowed, s_txt, masked_score)
                top = jnp.maximum(
                    jnp.max(s_img, axis=1, keepdims=True), jnp.max(s_txt, axis=1, keepdims=True)
                )
                p_img = jnp.exp(s_img - top)
                p_txt = jnp.exp(s_txt - top)
                total = jnp.sum(p_img, axis=1, keepdims=True) + jnp.sum(p_txt, axis=1, keepdims=True)
                acc = jnp.dot(
                    p_img.astype(jnp.bfloat16), v_img, preferred_element_type=jnp.float32
                ) + jnp.dot(p_txt.astype(jnp.bfloat16), v_txt, preferred_element_type=jnp.float32)
                out = jnp.where(in_head, acc / total, out)
            o_ref[r] = out.astype(o_ref.dtype)

    def run(q, kv, mask):
        return pl.pallas_call(
            kernel,
            out_shape=jax.ShapeDtypeStruct(q.shape, jnp.bfloat16),
            in_specs=[pl.BlockSpec(memory_space=pltpu.VMEM)] * 3,
            out_specs=pl.BlockSpec(memory_space=pltpu.VMEM),
        )(q, kv, mask)

    return run


def body(
    latent,
    img_hidden,
    txt_hidden,
    segments,
    timesteps,
    modulation,
    qk_gain,
    qkv_weight,
    text_weight,
    out_weight,
    expand_weight,
    contract_weight,
    final_weight,
):
    tokens_here = img_hidden.shape[1]
    requests = img_hidden.shape[2]
    feat_width = img_hidden.shape[3]
    head_size = qk_gain.shape[1]
    local_cols = qkv_weight.shape[2]
    heads_here = local_cols // head_size
    text_here = txt_hidden.shape[1]
    seq_size = lax.axis_size("z") * lax.axis_size("core")
    wgt_size = lax.axis_size("wgt")
    modulate = modulation[0]
    hidden = img_hidden[0].astype(jnp.float32)
    image_normed = (layer_norm(hidden) * (1.0 + modulate[:, 1]) + modulate[:, 0]).astype(
        jnp.bfloat16
    )
    row_count = tokens_here * requests
    token_rows = image_normed.reshape(row_count, feat_width)
    segment_row = segments[0]
    one_hot = (segment_row[:, None] == jnp.arange(requests, dtype=jnp.int32)[None, :]).astype(
        jnp.float32
    )
    text_mod = jnp.einsum("tr,rkd->tkd", one_hot, modulate[:, 3:5], precision=lax.Precision.HIGHEST)
    text_normed = (
        layer_norm(txt_hidden[0].astype(jnp.float32)) * (1.0 + text_mod[:, 1]) + text_mod[:, 0]
    ).astype(jnp.bfloat16)
    block_rows = qkv_weight.shape[1]
    padded_rows = block_rows + (-block_rows) % 8
    kinds = qkv_weight.shape[0] + text_weight.shape[0]
    all_weights = jnp.transpose(
        jnp.concatenate([qkv_weight, text_weight], axis=0), (1, 0, 2)
    ).reshape(block_rows, kinds * local_cols)
    all_weights = jnp.pad(all_weights, ((0, padded_rows - block_rows), (0, 0)))
    qkv_mine, qkv_other = half_gather(all_weights, 1)
    mlp_local = jnp.pad(
        jnp.stack([expand_weight, contract_weight.T], axis=0),
        ((0, 0), (0, padded_rows - block_rows), (0, 0)),
    )
    mlp_mine, mlp_other = half_gather(mlp_local, 2)
    out_full = lax.all_gather(out_weight, SEQ, axis=1, tiled=True)
    both_rows = jnp.concatenate([token_rows, text_normed], axis=0)
    both_count = both_rows.shape[0]
    both_rows = jnp.pad(
        both_rows.reshape(both_count, seq_size // 2, 2, block_rows),
        ((0, 0), (0, 0), (0, 0), (0, padded_rows - block_rows)),
    )
    term_mine = jnp.einsum(
        "rzcd,zcdn->rn", both_rows, qkv_mine, preferred_element_type=jnp.float32
    )
    term_other = jnp.einsum(
        "rzcd,zcdn->rn", both_rows, qkv_other, preferred_element_type=jnp.float32
    )
    first_core = lax.axis_index("core") == 0
    both_term = jnp.concatenate(
        [
            jnp.where(first_core, term_mine, term_other),
            jnp.where(first_core, term_other, term_mine),
        ],
        axis=1,
    ).reshape(both_count, kinds, local_cols)
    image_term = both_term[:row_count]
    text_term = both_term[row_count:]
    queries = head_norm(
        image_term[:, 0].reshape(tokens_here, requests, heads_here, head_size), qk_gain[0]
    ).astype(jnp.bfloat16)
    keys_img = head_norm(
        image_term[:, 1].reshape(tokens_here, requests, heads_here, head_size), qk_gain[1]
    ).astype(jnp.bfloat16)
    values_img = image_term[:, 2].reshape(tokens_here, requests, local_cols).astype(jnp.bfloat16)
    keys_txt = head_norm(
        text_term[:, 3].reshape(text_here, heads_here, head_size), qk_gain[1]
    ).astype(jnp.bfloat16)
    values_txt = text_term[:, 4].astype(jnp.bfloat16)
    image_pair = jnp.transpose(
        jnp.stack([keys_img.reshape(tokens_here, requests, local_cols), values_img], axis=0),
        (2, 0, 1, 3),
    ).reshape(requests * 2 * tokens_here, local_cols)
    text_pair = jnp.stack([keys_txt.reshape(text_here, local_cols), values_txt], axis=0).reshape(
        2 * text_here, local_cols
    )
    lanes = local_cols + (-local_cols) % 128
    image_pair = jnp.pad(image_pair, ((0, 0), (0, lanes - local_cols)))
    text_pair = jnp.pad(text_pair, ((0, 0), (0, lanes - local_cols)))
    owner_row = jnp.pad(
        segment_row.astype(jnp.float32).astype(jnp.bfloat16), (0, lanes - text_here)
    )[None, :]
    image_len = requests * 2 * tokens_here
    owner_at = image_len + 2 * text_here
    pad_rows = (-(owner_at + 1)) % 16
    shared = jnp.concatenate(
        [image_pair, text_pair, owner_row, jnp.zeros((pad_rows, lanes), jnp.bfloat16)], axis=0
    )
    shared_piece = lax.all_gather(shared, SEQ, axis=0, tiled=False)
    owner_piece = shared_piece[:, owner_at, :text_here].reshape(-1)
    request_ids = jnp.arange(requests, dtype=jnp.float32)
    text_mask = (owner_piece.astype(jnp.float32)[None, :] == request_ids[:, None]).astype(
        jnp.float32
    )
    query_block = jnp.pad(
        jnp.transpose(queries.reshape(tokens_here, requests, local_cols), (1, 0, 2)),
        ((0, 0), (0, 0), (0, lanes - local_cols)),
    )
    attend = make_attention(heads_here, head_size, image_len, text_here)
    attended = attend(query_block, shared_piece, text_mask)
    attended = jnp.transpose(attended[:, :, :local_cols], (1, 0, 2)).reshape(row_count, local_cols)
    share_rows = row_count // wgt_size
    mixed = group_sum(
        jnp.dot(attended, out_full, preferred_element_type=jnp.float32).astype(jnp.bfloat16),
        wgt_size,
    )
    tokens_out = share_rows // requests
    row_place = lax.axis_index("wgt") * share_rows
    base_rows = lax.dynamic_slice_in_dim(
        hidden.reshape(row_count, feat_width), row_place, share_rows, 0
    )
    residual = base_rows.reshape(tokens_out, requests, feat_width) + modulate[:, 2] * mixed.reshape(
        tokens_out, requests, feat_width
    )
    branch_in = (layer_norm(residual) * (1.0 + modulate[:, 6]) + modulate[:, 5]).astype(
        jnp.bfloat16
    )
    branch_rows = lax.all_to_all(
        jnp.broadcast_to(
            branch_in.reshape(1, share_rows, feat_width), (wgt_size, share_rows, feat_width)
        ),
        "wgt",
        0,
        0,
        tiled=True,
    ).reshape(row_count, feat_width)
    padded_rows_in = jnp.pad(
        branch_rows.reshape(row_count, seq_size // 2, 2, block_rows),
        ((0, 0), (0, 0), (0, 0), (0, padded_rows - block_rows)),
    )
    contracted = None
    for half in (mlp_mine, mlp_other):
        expanded = jnp.einsum(
            "rzcd,zcdf->rf", padded_rows_in, half[:, :, 0], preferred_element_type=jnp.float32
        )
        expanded = jax.nn.gelu(expanded, approximate=True).astype(jnp.bfloat16)
        part = jnp.einsum(
            "rf,zcdf->rzcd", expanded, half[:, :, 1], preferred_element_type=jnp.float32
        )
        contracted = part if contracted is None else contracted + part
    contracted = contracted[:, :, :, :block_rows].reshape(row_count, feat_width)
    branch = group_sum(contracted.astype(jnp.bfloat16), wgt_size)
    second = residual + modulate[:, 7] * branch.reshape(tokens_out, requests, feat_width)
    final_in = (layer_norm(second) * (1.0 + modulate[:, 9]) + modulate[:, 8]).astype(jnp.bfloat16)
    own_velocity = jnp.dot(
        final_in.reshape(share_rows, feat_width), final_weight, preferred_element_type=jnp.float32
    ).reshape(tokens_out, requests, -1)
    guide_side = lax.axis_index("cfg")
    guided_count = latent.shape[1]
    kept_rows = lax.dynamic_slice_in_dim(own_velocity, guide_side * guided_count, guided_count, 1)
    sent_rows = lax.dynamic_slice_in_dim(
        own_velocity, (1 - guide_side) * guided_count, guided_count, 1
    )
    partner_velocity = from_partner(sent_rows, "cfg", 0)
    is_first = guide_side == 0
    conditional = jnp.where(is_first, kept_rows, partner_velocity)
    unconditional = jnp.where(is_first, partner_velocity, kept_rows)
    velocity = unconditional + guidance_scale * (conditional - unconditional)
    step_size = sigma_of(timesteps + 1) - sigma_of(timesteps)
    step_here = lax.dynamic_slice_in_dim(step_size, guide_side * guided_count, guided_count, 0)
    next_latent = latent + step_here[None, :, None] * velocity
    return (velocity, next_latent)


def solution(mesh):
    cfg_n, seq_n, wgt_n = (mesh.shape[name] for name in ("cfg", "seq", "wgt"))
    fine = Mesh(mesh.devices.reshape(cfg_n, seq_n // 2, 2, wgt_n), ("cfg", "z", "core", "wgt"))
    return jax.shard_map(
        body,
        mesh=fine,
        in_specs=(
            P(("z", "core", "wgt"), "cfg", None),
            P("cfg", SEQ, None, None),
            P("cfg", SEQ, None),
            P("cfg", SEQ),
            P(),
            P("cfg", None, None, None),
            P(),
            P(None, SEQ, "wgt"),
            P(None, SEQ, "wgt"),
            P("wgt", SEQ),
            P(SEQ, "wgt"),
            P("wgt", SEQ),
            P(),
        ),
        out_specs=(P(("z", "core", "wgt"), "cfg", None), P(("z", "core", "wgt"), "cfg", None)),
        check_vma=False,
    )
```

```python
import jax
import jax.numpy as jnp
from jax import lax
from jax.experimental import pallas as pl
from jax.experimental.pallas import tpu as pltpu
from jax.sharding import PartitionSpec as P

STEPS = 28


guidance_scale = 3.5
flow_shift = 3.0
eps_norm = 1e-06
masked_score = -1e30


def from_partner(value, axis, bit):
    mask = 2**bit
    pairs = [(source, source ^ mask) for source in range(lax.axis_size(axis))]
    return lax.ppermute(value, axis, pairs)


def layer_norm(values):
    center = jnp.mean(values, axis=-1, keepdims=True)
    centred = values - center
    spread = jnp.mean(centred * centred, axis=-1, keepdims=True)
    return centred * lax.rsqrt(spread + eps_norm)


def head_norm(values, gain_row):
    power = jnp.mean(values * values, axis=-1, keepdims=True)
    return values * lax.rsqrt(power + eps_norm) * gain_row


def sigma_of(index_row):
    time_left = 1.0 - index_row.astype(jnp.float32) / STEPS
    return flow_shift * time_left / (1.0 + (flow_shift - 1.0) * time_left)


def group_sum(partial, groups):
    swapped = lax.all_to_all(partial, "wgt", 0, 0, tiled=True)
    rows = swapped.shape[0] // groups
    return jnp.sum(swapped.reshape(groups, rows, -1).astype(jnp.float32), axis=0)


def make_attention(heads, head_size, text_at, text_here):
    scale = head_size ** (-0.5)

    def kernel(q_ref, kv_ref, mask_ref, o_ref):
        requests, tokens, cols = q_ref.shape
        blocks = kv_ref.shape[0]
        lane = lax.broadcasted_iota(jnp.int32, (1, cols), 1)
        k_txt = kv_ref[:, text_at : text_at + text_here, :].reshape(blocks * text_here, cols)
        v_txt = kv_ref[:, text_at + text_here : text_at + 2 * text_here, :].reshape(
            blocks * text_here, cols
        )
        dims = (((1,), (1,)), ((), ()))
        for r in range(requests):
            q = q_ref[r].astype(jnp.float32)
            k_img = kv_ref[:, 2 * tokens * r : 2 * tokens * r + tokens, :].reshape(
                blocks * tokens, cols
            )
            v_img = kv_ref[:, 2 * tokens * r + tokens : 2 * tokens * (r + 1), :].reshape(
                blocks * tokens, cols
            )
            allowed = mask_ref[r : r + 1, :] > 0.5
            out = jnp.zeros((tokens, cols), jnp.float32)
            for h in range(heads):
                in_head = (lane >= h * head_size) & (lane < (h + 1) * head_size)
                qh = jnp.where(in_head, q, 0.0).astype(jnp.bfloat16)
                s_img = lax.dot_general(qh, k_img, dims, preferred_element_type=jnp.float32) * scale
                s_txt = lax.dot_general(qh, k_txt, dims, preferred_element_type=jnp.float32) * scale
                s_txt = jnp.where(allowed, s_txt, masked_score)
                top = jnp.maximum(
                    jnp.max(s_img, axis=1, keepdims=True), jnp.max(s_txt, axis=1, keepdims=True)
                )
                p_img = jnp.exp(s_img - top)
                p_txt = jnp.exp(s_txt - top)
                total = jnp.sum(p_img, axis=1, keepdims=True) + jnp.sum(p_txt, axis=1, keepdims=True)
                acc = jnp.dot(
                    p_img.astype(jnp.bfloat16), v_img, preferred_element_type=jnp.float32
                ) + jnp.dot(p_txt.astype(jnp.bfloat16), v_txt, preferred_element_type=jnp.float32)
                out = jnp.where(in_head, acc / total, out)
            o_ref[r] = out.astype(o_ref.dtype)

    def run(q, kv, mask):
        return pl.pallas_call(
            kernel,
            out_shape=jax.ShapeDtypeStruct(q.shape, jnp.bfloat16),
            in_specs=[pl.BlockSpec(memory_space=pltpu.VMEM)] * 3,
            out_specs=pl.BlockSpec(memory_space=pltpu.VMEM),
        )(q, kv, mask)

    return run


def body(
    latent,
    img_hidden,
    txt_hidden,
    segments,
    timesteps,
    modulation,
    qk_gain,
    qkv_weight,
    text_weight,
    out_weight,
    expand_weight,
    contract_weight,
    final_weight,
):
    tokens_here = img_hidden.shape[1]
    requests = img_hidden.shape[2]
    feat_width = img_hidden.shape[3]
    head_size = qk_gain.shape[1]
    local_cols = qkv_weight.shape[2]
    heads_here = local_cols // head_size
    text_here = txt_hidden.shape[1]
    seq_size = lax.axis_size("seq")
    wgt_size = lax.axis_size("wgt")
    modulate = modulation[0]
    hidden = img_hidden[0].astype(jnp.float32)
    image_normed = (layer_norm(hidden) * (1.0 + modulate[:, 1]) + modulate[:, 0]).astype(
        jnp.bfloat16
    )
    row_count = tokens_here * requests
    token_rows = image_normed.reshape(row_count, feat_width)
    segment_row = segments[0]
    one_hot = (segment_row[:, None] == jnp.arange(requests, dtype=jnp.int32)[None, :]).astype(
        jnp.float32
    )
    text_mod = jnp.einsum("tr,rkd->tkd", one_hot, modulate[:, 3:5], precision=lax.Precision.HIGHEST)
    text_normed = (
        layer_norm(txt_hidden[0].astype(jnp.float32)) * (1.0 + text_mod[:, 1]) + text_mod[:, 0]
    ).astype(jnp.bfloat16)
    block_rows = qkv_weight.shape[1]
    padded_rows = block_rows + (-block_rows) % 8
    kinds = qkv_weight.shape[0] + text_weight.shape[0]
    all_weights = jnp.transpose(
        jnp.concatenate([qkv_weight, text_weight], axis=0), (1, 0, 2)
    ).reshape(block_rows, kinds * local_cols)
    all_weights = jnp.pad(all_weights, ((0, padded_rows - block_rows), (0, 0)))
    piece = lax.all_gather(all_weights, "seq", axis=0, tiled=False)
    mlp_local = jnp.pad(
        jnp.stack([expand_weight, contract_weight.T], axis=0),
        ((0, 0), (0, padded_rows - block_rows), (0, 0)),
    )
    mlp_full = lax.all_gather(mlp_local, "seq", axis=0, tiled=False)
    out_full = lax.all_gather(out_weight, "seq", axis=1, tiled=True)
    both_rows = jnp.concatenate([token_rows, text_normed], axis=0)
    both_count = both_rows.shape[0]
    both_rows = jnp.pad(
        both_rows.reshape(both_count, seq_size, block_rows),
        ((0, 0), (0, 0), (0, padded_rows - block_rows)),
    )
    both_term = jnp.einsum(
        "rsd,sdn->rn", both_rows, piece, preferred_element_type=jnp.float32
    ).reshape(both_count, kinds, local_cols)
    image_term = both_term[:row_count]
    text_term = both_term[row_count:]
    queries = head_norm(
        image_term[:, 0].reshape(tokens_here, requests, heads_here, head_size), qk_gain[0]
    ).astype(jnp.bfloat16)
    keys_img = head_norm(
        image_term[:, 1].reshape(tokens_here, requests, heads_here, head_size), qk_gain[1]
    ).astype(jnp.bfloat16)
    values_img = image_term[:, 2].reshape(tokens_here, requests, local_cols).astype(jnp.bfloat16)
    keys_txt = head_norm(
        text_term[:, 3].reshape(text_here, heads_here, head_size), qk_gain[1]
    ).astype(jnp.bfloat16)
    values_txt = text_term[:, 4].astype(jnp.bfloat16)
    image_pair = jnp.transpose(
        jnp.stack([keys_img.reshape(tokens_here, requests, local_cols), values_img], axis=0),
        (2, 0, 1, 3),
    ).reshape(requests * 2 * tokens_here, local_cols)
    text_pair = jnp.stack([keys_txt.reshape(text_here, local_cols), values_txt], axis=0).reshape(
        2 * text_here, local_cols
    )
    lanes = local_cols + (-local_cols) % 128
    image_pair = jnp.pad(image_pair, ((0, 0), (0, lanes - local_cols)))
    text_pair = jnp.pad(text_pair, ((0, 0), (0, lanes - local_cols)))
    owner_row = jnp.pad(
        segment_row.astype(jnp.float32).astype(jnp.bfloat16), (0, lanes - text_here)
    )[None, :]
    image_len = requests * 2 * tokens_here
    owner_at = image_len + 2 * text_here
    pad_rows = (-(owner_at + 1)) % 16
    shared = jnp.concatenate(
        [image_pair, text_pair, owner_row, jnp.zeros((pad_rows, lanes), jnp.bfloat16)], axis=0
    )
    shared_piece = lax.all_gather(shared, "seq", axis=0, tiled=False)
    owner_piece = shared_piece[:, owner_at, :text_here].reshape(-1)
    request_ids = jnp.arange(requests, dtype=jnp.float32)
    text_mask = (owner_piece.astype(jnp.float32)[None, :] == request_ids[:, None]).astype(
        jnp.float32
    )
    query_block = jnp.pad(
        jnp.transpose(queries.reshape(tokens_here, requests, local_cols), (1, 0, 2)),
        ((0, 0), (0, 0), (0, lanes - local_cols)),
    )
    attend = make_attention(heads_here, head_size, image_len, text_here)
    attended = attend(query_block, shared_piece, text_mask)
    attended = jnp.transpose(attended[:, :, :local_cols], (1, 0, 2)).reshape(row_count, local_cols)
    share_rows = row_count // wgt_size
    mixed = group_sum(
        jnp.dot(attended, out_full, preferred_element_type=jnp.float32).astype(jnp.bfloat16),
        wgt_size,
    )
    tokens_out = share_rows // requests
    row_place = lax.axis_index("wgt") * share_rows
    base_rows = lax.dynamic_slice_in_dim(
        hidden.reshape(row_count, feat_width), row_place, share_rows, 0
    )
    residual = base_rows.reshape(tokens_out, requests, feat_width) + modulate[:, 2] * mixed.reshape(
        tokens_out, requests, feat_width
    )
    branch_in = (layer_norm(residual) * (1.0 + modulate[:, 6]) + modulate[:, 5]).astype(
        jnp.bfloat16
    )
    branch_rows = lax.all_to_all(
        jnp.broadcast_to(
            branch_in.reshape(1, share_rows, feat_width), (wgt_size, share_rows, feat_width)
        ),
        "wgt",
        0,
        0,
        tiled=True,
    ).reshape(row_count, feat_width)
    padded_rows_in = jnp.pad(
        branch_rows.reshape(row_count, seq_size, block_rows),
        ((0, 0), (0, 0), (0, padded_rows - block_rows)),
    )
    expanded = jnp.einsum(
        "rsd,sdf->rf", padded_rows_in, mlp_full[:, 0], preferred_element_type=jnp.float32
    )
    expanded = jax.nn.gelu(expanded, approximate=True).astype(jnp.bfloat16)
    contracted = jnp.einsum(
        "rf,sdf->rsd", expanded, mlp_full[:, 1], preferred_element_type=jnp.float32
    )[:, :, :block_rows].reshape(row_count, feat_width)
    branch = group_sum(contracted.astype(jnp.bfloat16), wgt_size)
    second = residual + modulate[:, 7] * branch.reshape(tokens_out, requests, feat_width)
    final_in = (layer_norm(second) * (1.0 + modulate[:, 9]) + modulate[:, 8]).astype(jnp.bfloat16)
    own_velocity = jnp.dot(
        final_in.reshape(share_rows, feat_width), final_weight, preferred_element_type=jnp.float32
    ).reshape(tokens_out, requests, -1)
    guide_side = lax.axis_index("cfg")
    guided_count = latent.shape[1]
    kept_rows = lax.dynamic_slice_in_dim(own_velocity, guide_side * guided_count, guided_count, 1)
    sent_rows = lax.dynamic_slice_in_dim(
        own_velocity, (1 - guide_side) * guided_count, guided_count, 1
    )
    partner_velocity = from_partner(sent_rows, "cfg", 0)
    is_first = guide_side == 0
    conditional = jnp.where(is_first, kept_rows, partner_velocity)
    unconditional = jnp.where(is_first, partner_velocity, kept_rows)
    velocity = unconditional + guidance_scale * (conditional - unconditional)
    step_size = sigma_of(timesteps + 1) - sigma_of(timesteps)
    step_here = lax.dynamic_slice_in_dim(step_size, guide_side * guided_count, guided_count, 0)
    next_latent = latent + step_here[None, :, None] * velocity
    return (velocity, next_latent)


def solution(mesh):
    return jax.shard_map(
        body,
        mesh=mesh,
        in_specs=(
            P(("seq", "wgt"), "cfg", None),
            P("cfg", "seq", None, None),
            P("cfg", "seq", None),
            P("cfg", "seq"),
            P(),
            P("cfg", None, None, None),
            P(),
            P(None, "seq", "wgt"),
            P(None, "seq", "wgt"),
            P("wgt", "seq"),
            P("seq", "wgt"),
            P("wgt", "seq"),
            P(),
        ),
        out_specs=(P(("seq", "wgt"), "cfg", None), P(("seq", "wgt"), "cfg", None)),
        check_vma=False,
    )
```

```python
import jax
import jax.numpy as jnp
from jax import lax
from jax.experimental import pallas as pl
from jax.experimental.pallas import tpu as pltpu
from jax.sharding import PartitionSpec as P

STEPS = 28


guidance_scale = 3.5
flow_shift = 3.0
eps_norm = 1e-06
masked_score = -1e30


def from_partner(value, axis, bit):
    mask = 2**bit
    pairs = [(source, source ^ mask) for source in range(lax.axis_size(axis))]
    return lax.ppermute(value, axis, pairs)


def layer_norm(values):
    center = jnp.mean(values, axis=-1, keepdims=True)
    centred = values - center
    spread = jnp.mean(centred * centred, axis=-1, keepdims=True)
    return centred * lax.rsqrt(spread + eps_norm)


def head_norm(values, gain_row):
    power = jnp.mean(values * values, axis=-1, keepdims=True)
    return values * lax.rsqrt(power + eps_norm) * gain_row


def sigma_of(index_row):
    time_left = 1.0 - index_row.astype(jnp.float32) / STEPS
    return flow_shift * time_left / (1.0 + (flow_shift - 1.0) * time_left)


def permute_sum(partial, groups):
    rows = partial.shape[0] // groups
    chunks = partial.reshape(groups, rows, -1)
    here = lax.axis_index("wgt")
    total = lax.dynamic_index_in_dim(chunks, here, 0, keepdims=False).astype(jnp.float32)
    for shift in range(1, groups):
        sent = lax.dynamic_index_in_dim(chunks, (here + shift) % groups, 0, keepdims=False)
        pairs = [(source, (source + shift) % groups) for source in range(groups)]
        total = total + lax.ppermute(sent, "wgt", pairs).astype(jnp.float32)
    return total


def group_sum(partial, groups):
    swapped = lax.all_to_all(partial, "wgt", 0, 0, tiled=True)
    rows = swapped.shape[0] // groups
    return jnp.sum(swapped.reshape(groups, rows, -1).astype(jnp.float32), axis=0)


def make_attention(heads, head_size, text_at, text_here):
    scale = head_size ** (-0.5)

    def kernel(q_ref, kv_ref, mask_ref, o_ref):
        requests, tokens, cols = q_ref.shape
        blocks = kv_ref.shape[0]
        lane = lax.broadcasted_iota(jnp.int32, (1, cols), 1)
        k_txt = kv_ref[:, text_at : text_at + text_here, :].reshape(blocks * text_here, cols)
        v_txt = kv_ref[:, text_at + text_here : text_at + 2 * text_here, :].reshape(
            blocks * text_here, cols
        )
        dims = (((1,), (1,)), ((), ()))
        for r in range(requests):
            q = q_ref[r].astype(jnp.float32)
            k_img = kv_ref[:, 2 * tokens * r : 2 * tokens * r + tokens, :].reshape(
                blocks * tokens, cols
            )
            v_img = kv_ref[:, 2 * tokens * r + tokens : 2 * tokens * (r + 1), :].reshape(
                blocks * tokens, cols
            )
            allowed = mask_ref[r : r + 1, :] > 0.5
            out = jnp.zeros((tokens, cols), jnp.float32)
            for h in range(heads):
                in_head = (lane >= h * head_size) & (lane < (h + 1) * head_size)
                qh = jnp.where(in_head, q, 0.0).astype(jnp.bfloat16)
                s_img = lax.dot_general(qh, k_img, dims, preferred_element_type=jnp.float32) * scale
                s_txt = lax.dot_general(qh, k_txt, dims, preferred_element_type=jnp.float32) * scale
                s_txt = jnp.where(allowed, s_txt, masked_score)
                top = jnp.maximum(
                    jnp.max(s_img, axis=1, keepdims=True), jnp.max(s_txt, axis=1, keepdims=True)
                )
                p_img = jnp.exp(s_img - top)
                p_txt = jnp.exp(s_txt - top)
                total = jnp.sum(p_img, axis=1, keepdims=True) + jnp.sum(p_txt, axis=1, keepdims=True)
                acc = jnp.dot(
                    p_img.astype(jnp.bfloat16), v_img, preferred_element_type=jnp.float32
                ) + jnp.dot(p_txt.astype(jnp.bfloat16), v_txt, preferred_element_type=jnp.float32)
                out = jnp.where(in_head, acc / total, out)
            o_ref[r] = out.astype(o_ref.dtype)

    def run(q, kv, mask):
        return pl.pallas_call(
            kernel,
            out_shape=jax.ShapeDtypeStruct(q.shape, jnp.bfloat16),
            in_specs=[pl.BlockSpec(memory_space=pltpu.VMEM)] * 3,
            out_specs=pl.BlockSpec(memory_space=pltpu.VMEM),
        )(q, kv, mask)

    return run


def body(
    latent,
    img_hidden,
    txt_hidden,
    segments,
    timesteps,
    modulation,
    qk_gain,
    qkv_weight,
    text_weight,
    out_weight,
    expand_weight,
    contract_weight,
    final_weight,
):
    tokens_here = img_hidden.shape[1]
    requests = img_hidden.shape[2]
    feat_width = img_hidden.shape[3]
    head_size = qk_gain.shape[1]
    local_cols = qkv_weight.shape[2]
    heads_here = local_cols // head_size
    text_here = txt_hidden.shape[1]
    seq_size = lax.axis_size("seq")
    wgt_size = lax.axis_size("wgt")
    modulate = modulation[0]
    hidden = img_hidden[0].astype(jnp.float32)
    image_normed = (layer_norm(hidden) * (1.0 + modulate[:, 1]) + modulate[:, 0]).astype(
        jnp.bfloat16
    )
    row_count = tokens_here * requests
    token_rows = image_normed.reshape(row_count, feat_width)
    segment_row = segments[0]
    one_hot = (segment_row[:, None] == jnp.arange(requests, dtype=jnp.int32)[None, :]).astype(
        jnp.float32
    )
    text_mod = jnp.einsum("tr,rkd->tkd", one_hot, modulate[:, 3:5], precision=lax.Precision.HIGHEST)
    text_normed = (
        layer_norm(txt_hidden[0].astype(jnp.float32)) * (1.0 + text_mod[:, 1]) + text_mod[:, 0]
    ).astype(jnp.bfloat16)
    block_rows = qkv_weight.shape[1]
    padded_rows = block_rows + (-block_rows) % 8
    kinds = qkv_weight.shape[0] + text_weight.shape[0]
    all_weights = jnp.transpose(
        jnp.concatenate([qkv_weight, text_weight], axis=0), (1, 0, 2)
    ).reshape(block_rows, kinds * local_cols)
    all_weights = jnp.pad(all_weights, ((0, padded_rows - block_rows), (0, 0)))
    piece = lax.all_gather(all_weights, "seq", axis=0, tiled=False)
    mlp_local = jnp.pad(
        jnp.stack([expand_weight, contract_weight.T], axis=0),
        ((0, 0), (0, padded_rows - block_rows), (0, 0)),
    )
    mlp_full = lax.all_gather(mlp_local, "seq", axis=0, tiled=False)
    out_full = lax.all_gather(out_weight, "seq", axis=1, tiled=True)
    both_rows = jnp.concatenate([token_rows, text_normed], axis=0)
    both_count = both_rows.shape[0]
    both_rows = jnp.pad(
        both_rows.reshape(both_count, seq_size, block_rows),
        ((0, 0), (0, 0), (0, padded_rows - block_rows)),
    )
    both_term = jnp.einsum(
        "rsd,sdn->rn", both_rows, piece, preferred_element_type=jnp.float32
    ).reshape(both_count, kinds, local_cols)
    image_term = both_term[:row_count]
    text_term = both_term[row_count:]
    queries = head_norm(
        image_term[:, 0].reshape(tokens_here, requests, heads_here, head_size), qk_gain[0]
    ).astype(jnp.bfloat16)
    keys_img = head_norm(
        image_term[:, 1].reshape(tokens_here, requests, heads_here, head_size), qk_gain[1]
    ).astype(jnp.bfloat16)
    values_img = image_term[:, 2].reshape(tokens_here, requests, local_cols).astype(jnp.bfloat16)
    keys_txt = head_norm(
        text_term[:, 3].reshape(text_here, heads_here, head_size), qk_gain[1]
    ).astype(jnp.bfloat16)
    values_txt = text_term[:, 4].astype(jnp.bfloat16)
    image_pair = jnp.transpose(
        jnp.stack([keys_img.reshape(tokens_here, requests, local_cols), values_img], axis=0),
        (2, 0, 1, 3),
    ).reshape(requests * 2 * tokens_here, local_cols)
    text_pair = jnp.stack([keys_txt.reshape(text_here, local_cols), values_txt], axis=0).reshape(
        2 * text_here, local_cols
    )
    lanes = local_cols + (-local_cols) % 128
    image_pair = jnp.pad(image_pair, ((0, 0), (0, lanes - local_cols)))
    text_pair = jnp.pad(text_pair, ((0, 0), (0, lanes - local_cols)))
    owner_row = jnp.pad(
        segment_row.astype(jnp.float32).astype(jnp.bfloat16), (0, lanes - text_here)
    )[None, :]
    image_len = requests * 2 * tokens_here
    owner_at = image_len + 2 * text_here
    pad_rows = (-(owner_at + 1)) % 16
    shared = jnp.concatenate(
        [image_pair, text_pair, owner_row, jnp.zeros((pad_rows, lanes), jnp.bfloat16)], axis=0
    )
    shared_piece = lax.all_gather(shared, "seq", axis=0, tiled=False)
    owner_piece = shared_piece[:, owner_at, :text_here].reshape(-1)
    request_ids = jnp.arange(requests, dtype=jnp.float32)
    text_mask = (owner_piece.astype(jnp.float32)[None, :] == request_ids[:, None]).astype(
        jnp.float32
    )
    query_block = jnp.pad(
        jnp.transpose(queries.reshape(tokens_here, requests, local_cols), (1, 0, 2)),
        ((0, 0), (0, 0), (0, lanes - local_cols)),
    )
    attend = make_attention(heads_here, head_size, image_len, text_here)
    attended = attend(query_block, shared_piece, text_mask)
    attended = jnp.transpose(attended[:, :, :local_cols], (1, 0, 2)).reshape(row_count, local_cols)
    share_rows = row_count // wgt_size
    mixed = group_sum(
        jnp.dot(attended, out_full, preferred_element_type=jnp.float32).astype(jnp.bfloat16),
        wgt_size,
    )
    tokens_out = share_rows // requests
    row_place = lax.axis_index("wgt") * share_rows
    base_rows = lax.dynamic_slice_in_dim(
        hidden.reshape(row_count, feat_width), row_place, share_rows, 0
    )
    residual = base_rows.reshape(tokens_out, requests, feat_width) + modulate[:, 2] * mixed.reshape(
        tokens_out, requests, feat_width
    )
    branch_in = (layer_norm(residual) * (1.0 + modulate[:, 6]) + modulate[:, 5]).astype(
        jnp.bfloat16
    )
    branch_rows = lax.all_to_all(
        jnp.broadcast_to(
            branch_in.reshape(1, share_rows, feat_width), (wgt_size, share_rows, feat_width)
        ),
        "wgt",
        0,
        0,
        tiled=True,
    ).reshape(row_count, feat_width)
    padded_rows_in = jnp.pad(
        branch_rows.reshape(row_count, seq_size, block_rows),
        ((0, 0), (0, 0), (0, padded_rows - block_rows)),
    )
    expanded = jnp.einsum(
        "rsd,sdf->rf", padded_rows_in, mlp_full[:, 0], preferred_element_type=jnp.float32
    )
    expanded = jax.nn.gelu(expanded, approximate=True).astype(jnp.bfloat16)
    contracted = jnp.einsum(
        "rf,sdf->rsd", expanded, mlp_full[:, 1], preferred_element_type=jnp.float32
    )[:, :, :block_rows].reshape(row_count, feat_width)
    branch = permute_sum(contracted.astype(jnp.bfloat16), wgt_size)
    second = residual + modulate[:, 7] * branch.reshape(tokens_out, requests, feat_width)
    final_in = (layer_norm(second) * (1.0 + modulate[:, 9]) + modulate[:, 8]).astype(jnp.bfloat16)
    own_velocity = jnp.dot(
        final_in.reshape(share_rows, feat_width), final_weight, preferred_element_type=jnp.float32
    ).reshape(tokens_out, requests, -1)
    guide_side = lax.axis_index("cfg")
    guided_count = latent.shape[1]
    kept_rows = lax.dynamic_slice_in_dim(own_velocity, guide_side * guided_count, guided_count, 1)
    sent_rows = lax.dynamic_slice_in_dim(
        own_velocity, (1 - guide_side) * guided_count, guided_count, 1
    )
    partner_velocity = from_partner(sent_rows, "cfg", 0)
    is_first = guide_side == 0
    conditional = jnp.where(is_first, kept_rows, partner_velocity)
    unconditional = jnp.where(is_first, partner_velocity, kept_rows)
    velocity = unconditional + guidance_scale * (conditional - unconditional)
    step_size = sigma_of(timesteps + 1) - sigma_of(timesteps)
    step_here = lax.dynamic_slice_in_dim(step_size, guide_side * guided_count, guided_count, 0)
    next_latent = latent + step_here[None, :, None] * velocity
    return (velocity, next_latent)


def solution(mesh):
    return jax.shard_map(
        body,
        mesh=mesh,
        in_specs=(
            P(("seq", "wgt"), "cfg", None),
            P("cfg", "seq", None, None),
            P("cfg", "seq", None),
            P("cfg", "seq"),
            P(),
            P("cfg", None, None, None),
            P(),
            P(None, "seq", "wgt"),
            P(None, "seq", "wgt"),
            P("wgt", "seq"),
            P("seq", "wgt"),
            P("wgt", "seq"),
            P(),
        ),
        out_specs=(P(("seq", "wgt"), "cfg", None), P(("seq", "wgt"), "cfg", None)),
        check_vma=False,
    )
```

```python
import jax
import jax.numpy as jnp
from jax import lax
from jax.experimental import pallas as pl
from jax.experimental.pallas import tpu as pltpu
from jax.sharding import PartitionSpec as P

STEPS = 28


guidance_scale = 3.5
flow_shift = 3.0
eps_norm = 1e-06
masked_score = -1e30


def from_partner(value, axis, bit):
    mask = 2**bit
    pairs = [(source, source ^ mask) for source in range(lax.axis_size(axis))]
    return lax.ppermute(value, axis, pairs)


def layer_norm(values):
    center = jnp.mean(values, axis=-1, keepdims=True)
    centred = values - center
    spread = jnp.mean(centred * centred, axis=-1, keepdims=True)
    return centred * lax.rsqrt(spread + eps_norm)


def head_norm(values, gain_row):
    power = jnp.mean(values * values, axis=-1, keepdims=True)
    return values * lax.rsqrt(power + eps_norm) * gain_row


def sigma_of(index_row):
    time_left = 1.0 - index_row.astype(jnp.float32) / STEPS
    return flow_shift * time_left / (1.0 + (flow_shift - 1.0) * time_left)


def group_sum(partial, groups):
    swapped = lax.all_to_all(partial, "wgt", 0, 0, tiled=True)
    rows = swapped.shape[0] // groups
    return jnp.sum(swapped.reshape(groups, rows, -1).astype(jnp.float32), axis=0)


def make_attention(heads, head_size, text_at, text_here):
    scale = head_size ** (-0.5)

    def kernel(q_ref, kv_ref, mask_ref, o_ref):
        requests, tokens, cols = q_ref.shape
        blocks = kv_ref.shape[0]
        lane = lax.broadcasted_iota(jnp.int32, (1, cols), 1)
        k_txt = kv_ref[:, text_at : text_at + text_here, :].reshape(blocks * text_here, cols)
        v_txt = kv_ref[:, text_at + text_here : text_at + 2 * text_here, :].reshape(
            blocks * text_here, cols
        )
        dims = (((1,), (1,)), ((), ()))
        for r in range(requests):
            q = q_ref[r].astype(jnp.float32)
            k_img = kv_ref[:, 2 * tokens * r : 2 * tokens * r + tokens, :].reshape(
                blocks * tokens, cols
            )
            v_img = kv_ref[:, 2 * tokens * r + tokens : 2 * tokens * (r + 1), :].reshape(
                blocks * tokens, cols
            )
            allowed = mask_ref[r : r + 1, :] > 0.5
            out = jnp.zeros((tokens, cols), jnp.float32)
            for h in range(heads):
                in_head = (lane >= h * head_size) & (lane < (h + 1) * head_size)
                qh = jnp.where(in_head, q, 0.0).astype(jnp.bfloat16)
                s_img = lax.dot_general(qh, k_img, dims, preferred_element_type=jnp.float32) * scale
                s_txt = lax.dot_general(qh, k_txt, dims, preferred_element_type=jnp.float32) * scale
                s_txt = jnp.where(allowed, s_txt, masked_score)
                top = jnp.maximum(
                    jnp.max(s_img, axis=1, keepdims=True), jnp.max(s_txt, axis=1, keepdims=True)
                )
                p_img = jnp.exp(s_img - top)
                p_txt = jnp.exp(s_txt - top)
                total = jnp.sum(p_img, axis=1, keepdims=True) + jnp.sum(p_txt, axis=1, keepdims=True)
                acc = jnp.dot(
                    p_img.astype(jnp.bfloat16), v_img, preferred_element_type=jnp.float32
                ) + jnp.dot(p_txt.astype(jnp.bfloat16), v_txt, preferred_element_type=jnp.float32)
                out = jnp.where(in_head, acc / total, out)
            o_ref[r] = out.astype(o_ref.dtype)

    def run(q, kv, mask):
        return pl.pallas_call(
            kernel,
            out_shape=jax.ShapeDtypeStruct(q.shape, jnp.bfloat16),
            in_specs=[pl.BlockSpec(memory_space=pltpu.VMEM)] * 3,
            out_specs=pl.BlockSpec(memory_space=pltpu.VMEM),
        )(q, kv, mask)

    return run


def body(
    latent,
    img_hidden,
    txt_hidden,
    segments,
    timesteps,
    modulation,
    qk_gain,
    qkv_weight,
    text_weight,
    out_weight,
    expand_weight,
    contract_weight,
    final_weight,
):
    tokens_here = img_hidden.shape[1]
    requests = img_hidden.shape[2]
    feat_width = img_hidden.shape[3]
    head_size = qk_gain.shape[1]
    local_cols = qkv_weight.shape[2]
    heads_here = local_cols // head_size
    text_here = txt_hidden.shape[1]
    seq_size = lax.axis_size("seq")
    wgt_size = lax.axis_size("wgt")
    modulate = modulation[0]
    hidden = img_hidden[0].astype(jnp.float32)
    image_normed = (layer_norm(hidden) * (1.0 + modulate[:, 1]) + modulate[:, 0]).astype(
        jnp.bfloat16
    )
    row_count = tokens_here * requests
    token_rows = image_normed.reshape(row_count, feat_width)
    segment_row = segments[0]
    one_hot = (segment_row[:, None] == jnp.arange(requests, dtype=jnp.int32)[None, :]).astype(
        jnp.float32
    )
    text_mod = jnp.einsum("tr,rkd->tkd", one_hot, modulate[:, 3:5], precision=lax.Precision.HIGHEST)
    text_normed = (
        layer_norm(txt_hidden[0].astype(jnp.float32)) * (1.0 + text_mod[:, 1]) + text_mod[:, 0]
    ).astype(jnp.bfloat16)
    block_rows = qkv_weight.shape[1]
    padded_rows = block_rows + (-block_rows) % 8
    kinds = qkv_weight.shape[0] + text_weight.shape[0]
    all_weights = jnp.transpose(
        jnp.concatenate([qkv_weight, text_weight], axis=0), (1, 0, 2)
    ).reshape(block_rows, kinds * local_cols)
    all_weights = jnp.pad(all_weights, ((0, padded_rows - block_rows), (0, 0)))
    piece = lax.all_gather(all_weights, "seq", axis=0, tiled=False)
    mlp_local = jnp.pad(
        jnp.stack([expand_weight, contract_weight.T], axis=0),
        ((0, 0), (0, padded_rows - block_rows), (0, 0)),
    )
    mlp_full = lax.all_gather(mlp_local, "seq", axis=0, tiled=False)
    out_full = lax.all_gather(out_weight, "seq", axis=1, tiled=True)
    both_rows = jnp.concatenate([token_rows, text_normed], axis=0)
    both_count = both_rows.shape[0]
    both_rows = jnp.pad(
        both_rows.reshape(both_count, seq_size, block_rows),
        ((0, 0), (0, 0), (0, padded_rows - block_rows)),
    )
    both_term = jnp.einsum(
        "rsd,sdn->rn", both_rows, piece, preferred_element_type=jnp.float32
    ).reshape(both_count, kinds, local_cols)
    image_term = both_term[:row_count]
    text_term = both_term[row_count:]
    queries = head_norm(
        image_term[:, 0].reshape(tokens_here, requests, heads_here, head_size), qk_gain[0]
    ).astype(jnp.bfloat16)
    keys_img = head_norm(
        image_term[:, 1].reshape(tokens_here, requests, heads_here, head_size), qk_gain[1]
    ).astype(jnp.bfloat16)
    values_img = image_term[:, 2].reshape(tokens_here, requests, local_cols).astype(jnp.bfloat16)
    keys_txt = head_norm(
        text_term[:, 3].reshape(text_here, heads_here, head_size), qk_gain[1]
    ).astype(jnp.bfloat16)
    values_txt = text_term[:, 4].astype(jnp.bfloat16)
    image_pair = jnp.transpose(
        jnp.stack([keys_img.reshape(tokens_here, requests, local_cols), values_img], axis=0),
        (2, 0, 1, 3),
    ).reshape(requests * 2 * tokens_here, local_cols)
    text_pair = jnp.stack([keys_txt.reshape(text_here, local_cols), values_txt], axis=0).reshape(
        2 * text_here, local_cols
    )
    lanes = local_cols + (-local_cols) % 128
    image_pair = jnp.pad(image_pair, ((0, 0), (0, lanes - local_cols)))
    text_pair = jnp.pad(text_pair, ((0, 0), (0, lanes - local_cols)))
    owner_row = jnp.pad(
        segment_row.astype(jnp.float32).astype(jnp.bfloat16), (0, lanes - text_here)
    )[None, :]
    image_len = requests * 2 * tokens_here
    owner_at = image_len + 2 * text_here
    pad_rows = (-(owner_at + 1)) % 16
    shared = jnp.concatenate(
        [image_pair, text_pair, owner_row, jnp.zeros((pad_rows, lanes), jnp.bfloat16)], axis=0
    )
    shared_piece = lax.all_gather(shared, "seq", axis=0, tiled=False)
    owner_piece = shared_piece[:, owner_at, :text_here].reshape(-1)
    request_ids = jnp.arange(requests, dtype=jnp.float32)
    text_mask = (owner_piece.astype(jnp.float32)[None, :] == request_ids[:, None]).astype(
        jnp.float32
    )
    query_block = jnp.pad(
        jnp.transpose(queries.reshape(tokens_here, requests, local_cols), (1, 0, 2)),
        ((0, 0), (0, 0), (0, lanes - local_cols)),
    )
    attend = make_attention(heads_here, head_size, image_len, text_here)
    attended = attend(query_block, shared_piece, text_mask)
    attended = jnp.transpose(attended[:, :, :local_cols], (1, 0, 2)).reshape(row_count, local_cols)
    share_rows = row_count // wgt_size
    mixed = group_sum(
        jnp.dot(attended, out_full, preferred_element_type=jnp.float32).astype(jnp.bfloat16),
        wgt_size,
    )
    tokens_out = share_rows // requests
    row_place = lax.axis_index("wgt") * share_rows
    base_rows = lax.dynamic_slice_in_dim(
        hidden.reshape(row_count, feat_width), row_place, share_rows, 0
    )
    residual = base_rows.reshape(tokens_out, requests, feat_width) + modulate[:, 2] * mixed.reshape(
        tokens_out, requests, feat_width
    )
    branch_in = (layer_norm(residual) * (1.0 + modulate[:, 6]) + modulate[:, 5]).astype(
        jnp.bfloat16
    )
    branch_rows = lax.all_to_all(
        jnp.broadcast_to(
            branch_in.reshape(1, share_rows, feat_width), (wgt_size, share_rows, feat_width)
        ),
        "wgt",
        0,
        0,
        tiled=True,
    ).reshape(row_count, feat_width)
    padded_rows_in = jnp.pad(
        branch_rows.reshape(row_count, seq_size, block_rows),
        ((0, 0), (0, 0), (0, padded_rows - block_rows)),
    )
    expanded = jnp.einsum(
        "rsd,sdf->rf", padded_rows_in, mlp_full[:, 0], preferred_element_type=jnp.float32
    )
    expanded = jax.nn.gelu(expanded, approximate=True).astype(jnp.bfloat16)
    contracted = jnp.einsum(
        "rf,sdf->rsd", expanded, mlp_full[:, 1], preferred_element_type=jnp.float32
    ).astype(jnp.bfloat16)
    branch = group_sum(contracted.reshape(row_count, seq_size * padded_rows), wgt_size)
    branch = branch.reshape(share_rows, seq_size, padded_rows)[:, :, :block_rows].reshape(
        share_rows, feat_width
    )
    second = residual + modulate[:, 7] * branch.reshape(tokens_out, requests, feat_width)
    final_in = (layer_norm(second) * (1.0 + modulate[:, 9]) + modulate[:, 8]).astype(jnp.bfloat16)
    own_velocity = jnp.dot(
        final_in.reshape(share_rows, feat_width), final_weight, preferred_element_type=jnp.float32
    ).reshape(tokens_out, requests, -1)
    guide_side = lax.axis_index("cfg")
    guided_count = latent.shape[1]
    kept_rows = lax.dynamic_slice_in_dim(own_velocity, guide_side * guided_count, guided_count, 1)
    sent_rows = lax.dynamic_slice_in_dim(
        own_velocity, (1 - guide_side) * guided_count, guided_count, 1
    )
    partner_velocity = from_partner(sent_rows, "cfg", 0)
    is_first = guide_side == 0
    conditional = jnp.where(is_first, kept_rows, partner_velocity)
    unconditional = jnp.where(is_first, partner_velocity, kept_rows)
    velocity = unconditional + guidance_scale * (conditional - unconditional)
    step_size = sigma_of(timesteps + 1) - sigma_of(timesteps)
    step_here = lax.dynamic_slice_in_dim(step_size, guide_side * guided_count, guided_count, 0)
    next_latent = latent + step_here[None, :, None] * velocity
    return (velocity, next_latent)


def solution(mesh):
    return jax.shard_map(
        body,
        mesh=mesh,
        in_specs=(
            P(("seq", "wgt"), "cfg", None),
            P("cfg", "seq", None, None),
            P("cfg", "seq", None),
            P("cfg", "seq"),
            P(),
            P("cfg", None, None, None),
            P(),
            P(None, "seq", "wgt"),
            P(None, "seq", "wgt"),
            P("wgt", "seq"),
            P("seq", "wgt"),
            P("wgt", "seq"),
            P(),
        ),
        out_specs=(P(("seq", "wgt"), "cfg", None), P(("seq", "wgt"), "cfg", None)),
        check_vma=False,
    )
```

```python
import jax
import jax.numpy as jnp
from jax import lax
from jax.experimental import pallas as pl
from jax.experimental.pallas import tpu as pltpu
from jax.sharding import PartitionSpec as P

STEPS = 28


guidance_scale = 3.5
flow_shift = 3.0
eps_norm = 1e-06
masked_score = -1e30


def from_partner(value, axis, bit):
    mask = 2**bit
    pairs = [(source, source ^ mask) for source in range(lax.axis_size(axis))]
    return lax.ppermute(value, axis, pairs)


def layer_norm(values):
    center = jnp.mean(values, axis=-1, keepdims=True)
    centred = values - center
    spread = jnp.mean(centred * centred, axis=-1, keepdims=True)
    return centred * lax.rsqrt(spread + eps_norm)


def head_norm(values, gain_row):
    power = jnp.mean(values * values, axis=-1, keepdims=True)
    return values * lax.rsqrt(power + eps_norm) * gain_row


def sigma_of(index_row):
    time_left = 1.0 - index_row.astype(jnp.float32) / STEPS
    return flow_shift * time_left / (1.0 + (flow_shift - 1.0) * time_left)


def group_sum(partial, groups):
    swapped = lax.all_to_all(partial, "wgt", 0, 0, tiled=True)
    rows = swapped.shape[0] // groups
    return jnp.sum(swapped.reshape(groups, rows, -1).astype(jnp.float32), axis=0)


def make_attention(heads, head_size, text_at, text_here):
    scale = head_size ** (-0.5)

    def kernel(q_ref, kv_ref, mask_ref, o_ref):
        requests, tokens, cols = q_ref.shape
        blocks = kv_ref.shape[0]
        lane = lax.broadcasted_iota(jnp.int32, (1, cols), 1)
        k_txt = kv_ref[:, text_at : text_at + text_here, :].reshape(blocks * text_here, cols)
        v_txt = kv_ref[:, text_at + text_here : text_at + 2 * text_here, :].reshape(
            blocks * text_here, cols
        )
        dims = (((1,), (1,)), ((), ()))
        for r in range(requests):
            q = q_ref[r].astype(jnp.float32)
            k_img = kv_ref[:, 2 * tokens * r : 2 * tokens * r + tokens, :].reshape(
                blocks * tokens, cols
            )
            v_img = kv_ref[:, 2 * tokens * r + tokens : 2 * tokens * (r + 1), :].reshape(
                blocks * tokens, cols
            )
            allowed = mask_ref[r : r + 1, :] > 0.5
            out = jnp.zeros((tokens, cols), jnp.float32)
            for h in range(heads):
                in_head = (lane >= h * head_size) & (lane < (h + 1) * head_size)
                qh = jnp.where(in_head, q, 0.0).astype(jnp.bfloat16)
                s_img = lax.dot_general(qh, k_img, dims, preferred_element_type=jnp.float32) * scale
                s_txt = lax.dot_general(qh, k_txt, dims, preferred_element_type=jnp.float32) * scale
                s_txt = jnp.where(allowed, s_txt, masked_score)
                top = jnp.maximum(
                    jnp.max(s_img, axis=1, keepdims=True), jnp.max(s_txt, axis=1, keepdims=True)
                )
                p_img = jnp.exp(s_img - top)
                p_txt = jnp.exp(s_txt - top)
                total = jnp.sum(p_img, axis=1, keepdims=True) + jnp.sum(p_txt, axis=1, keepdims=True)
                acc = jnp.dot(
                    p_img.astype(jnp.bfloat16), v_img, preferred_element_type=jnp.float32
                ) + jnp.dot(p_txt.astype(jnp.bfloat16), v_txt, preferred_element_type=jnp.float32)
                out = jnp.where(in_head, acc / total, out)
            o_ref[r] = out.astype(o_ref.dtype)

    def run(q, kv, mask):
        return pl.pallas_call(
            kernel,
            out_shape=jax.ShapeDtypeStruct(q.shape, jnp.bfloat16),
            in_specs=[pl.BlockSpec(memory_space=pltpu.VMEM)] * 3,
            out_specs=pl.BlockSpec(memory_space=pltpu.VMEM),
        )(q, kv, mask)

    return run


def body(
    latent,
    img_hidden,
    txt_hidden,
    segments,
    timesteps,
    modulation,
    qk_gain,
    qkv_weight,
    text_weight,
    out_weight,
    expand_weight,
    contract_weight,
    final_weight,
):
    tokens_here = img_hidden.shape[1]
    requests = img_hidden.shape[2]
    feat_width = img_hidden.shape[3]
    head_size = qk_gain.shape[1]
    local_cols = qkv_weight.shape[2]
    heads_here = local_cols // head_size
    text_here = txt_hidden.shape[1]
    seq_size = lax.axis_size("seq")
    wgt_size = lax.axis_size("wgt")
    modulate = modulation[0]
    hidden = img_hidden[0].astype(jnp.float32)
    image_normed = (layer_norm(hidden) * (1.0 + modulate[:, 1]) + modulate[:, 0]).astype(
        jnp.bfloat16
    )
    row_count = tokens_here * requests
    token_rows = image_normed.reshape(row_count, feat_width)
    segment_row = segments[0]
    one_hot = (segment_row[:, None] == jnp.arange(requests, dtype=jnp.int32)[None, :]).astype(
        jnp.float32
    )
    text_mod = jnp.einsum("tr,rkd->tkd", one_hot, modulate[:, 3:5], precision=lax.Precision.HIGHEST)
    text_normed = (
        layer_norm(txt_hidden[0].astype(jnp.float32)) * (1.0 + text_mod[:, 1]) + text_mod[:, 0]
    ).astype(jnp.bfloat16)
    block_rows = qkv_weight.shape[1]
    padded_rows = block_rows + (-block_rows) % 8
    kinds = qkv_weight.shape[0] + text_weight.shape[0]
    all_weights = jnp.transpose(
        jnp.concatenate([qkv_weight, text_weight], axis=0), (1, 0, 2)
    ).reshape(block_rows, kinds * local_cols)
    all_weights = jnp.pad(all_weights, ((0, padded_rows - block_rows), (0, 0)))
    piece = lax.all_gather(all_weights, "seq", axis=0, tiled=False)
    mlp_local = jnp.pad(
        jnp.stack([expand_weight, contract_weight.T], axis=0),
        ((0, 0), (0, padded_rows - block_rows), (0, 0)),
    )
    mlp_full = lax.all_gather(mlp_local, "seq", axis=0, tiled=False)
    out_full = lax.all_gather(out_weight, "seq", axis=1, tiled=True)
    both_rows = jnp.concatenate([token_rows, text_normed], axis=0)
    both_count = both_rows.shape[0]
    both_cols = jnp.pad(
        both_rows.T.reshape(seq_size, block_rows, both_count),
        ((0, 0), (0, padded_rows - block_rows), (0, 0)),
    )
    both_term = jnp.einsum(
        "sdr,sdn->rn", both_cols, piece, preferred_element_type=jnp.float32
    ).reshape(both_count, kinds, local_cols)
    image_term = both_term[:row_count]
    text_term = both_term[row_count:]
    queries = head_norm(
        image_term[:, 0].reshape(tokens_here, requests, heads_here, head_size), qk_gain[0]
    ).astype(jnp.bfloat16)
    keys_img = head_norm(
        image_term[:, 1].reshape(tokens_here, requests, heads_here, head_size), qk_gain[1]
    ).astype(jnp.bfloat16)
    values_img = image_term[:, 2].reshape(tokens_here, requests, local_cols).astype(jnp.bfloat16)
    keys_txt = head_norm(
        text_term[:, 3].reshape(text_here, heads_here, head_size), qk_gain[1]
    ).astype(jnp.bfloat16)
    values_txt = text_term[:, 4].astype(jnp.bfloat16)
    image_pair = jnp.transpose(
        jnp.stack([keys_img.reshape(tokens_here, requests, local_cols), values_img], axis=0),
        (2, 0, 1, 3),
    ).reshape(requests * 2 * tokens_here, local_cols)
    text_pair = jnp.stack([keys_txt.reshape(text_here, local_cols), values_txt], axis=0).reshape(
        2 * text_here, local_cols
    )
    lanes = local_cols + (-local_cols) % 128
    image_pair = jnp.pad(image_pair, ((0, 0), (0, lanes - local_cols)))
    text_pair = jnp.pad(text_pair, ((0, 0), (0, lanes - local_cols)))
    owner_row = jnp.pad(
        segment_row.astype(jnp.float32).astype(jnp.bfloat16), (0, lanes - text_here)
    )[None, :]
    image_len = requests * 2 * tokens_here
    owner_at = image_len + 2 * text_here
    pad_rows = (-(owner_at + 1)) % 16
    shared = jnp.concatenate(
        [image_pair, text_pair, owner_row, jnp.zeros((pad_rows, lanes), jnp.bfloat16)], axis=0
    )
    shared_piece = lax.all_gather(shared, "seq", axis=0, tiled=False)
    owner_piece = shared_piece[:, owner_at, :text_here].reshape(-1)
    request_ids = jnp.arange(requests, dtype=jnp.float32)
    text_mask = (owner_piece.astype(jnp.float32)[None, :] == request_ids[:, None]).astype(
        jnp.float32
    )
    query_block = jnp.pad(
        jnp.transpose(queries.reshape(tokens_here, requests, local_cols), (1, 0, 2)),
        ((0, 0), (0, 0), (0, lanes - local_cols)),
    )
    attend = make_attention(heads_here, head_size, image_len, text_here)
    attended = attend(query_block, shared_piece, text_mask)
    attended = jnp.transpose(attended[:, :, :local_cols], (1, 0, 2)).reshape(row_count, local_cols)
    share_rows = row_count // wgt_size
    mixed = group_sum(
        jnp.dot(attended, out_full, preferred_element_type=jnp.float32).astype(jnp.bfloat16),
        wgt_size,
    )
    tokens_out = share_rows // requests
    row_place = lax.axis_index("wgt") * share_rows
    base_rows = lax.dynamic_slice_in_dim(
        hidden.reshape(row_count, feat_width), row_place, share_rows, 0
    )
    residual = base_rows.reshape(tokens_out, requests, feat_width) + modulate[:, 2] * mixed.reshape(
        tokens_out, requests, feat_width
    )
    branch_in = (layer_norm(residual) * (1.0 + modulate[:, 6]) + modulate[:, 5]).astype(
        jnp.bfloat16
    )
    branch_rows = lax.all_to_all(
        jnp.broadcast_to(
            branch_in.reshape(1, share_rows, feat_width), (wgt_size, share_rows, feat_width)
        ),
        "wgt",
        0,
        0,
        tiled=True,
    ).reshape(row_count, feat_width)
    padded_rows_in = jnp.pad(
        branch_rows.reshape(row_count, seq_size, block_rows),
        ((0, 0), (0, 0), (0, padded_rows - block_rows)),
    )
    expanded = jnp.einsum(
        "rsd,sdf->rf", padded_rows_in, mlp_full[:, 0], preferred_element_type=jnp.float32
    )
    expanded = jax.nn.gelu(expanded, approximate=True).astype(jnp.bfloat16)
    contracted = jnp.einsum(
        "rf,sdf->rsd", expanded, mlp_full[:, 1], preferred_element_type=jnp.float32
    ).astype(jnp.bfloat16)
    branch = group_sum(contracted.reshape(row_count, seq_size * padded_rows), wgt_size)
    branch = branch.reshape(share_rows, seq_size, padded_rows)[:, :, :block_rows].reshape(
        share_rows, feat_width
    )
    second = residual + modulate[:, 7] * branch.reshape(tokens_out, requests, feat_width)
    final_in = (layer_norm(second) * (1.0 + modulate[:, 9]) + modulate[:, 8]).astype(jnp.bfloat16)
    own_velocity = jnp.dot(
        final_in.reshape(share_rows, feat_width), final_weight, preferred_element_type=jnp.float32
    ).reshape(tokens_out, requests, -1)
    guide_side = lax.axis_index("cfg")
    guided_count = latent.shape[1]
    kept_rows = lax.dynamic_slice_in_dim(own_velocity, guide_side * guided_count, guided_count, 1)
    sent_rows = lax.dynamic_slice_in_dim(
        own_velocity, (1 - guide_side) * guided_count, guided_count, 1
    )
    partner_velocity = from_partner(sent_rows, "cfg", 0)
    is_first = guide_side == 0
    conditional = jnp.where(is_first, kept_rows, partner_velocity)
    unconditional = jnp.where(is_first, partner_velocity, kept_rows)
    velocity = unconditional + guidance_scale * (conditional - unconditional)
    step_size = sigma_of(timesteps + 1) - sigma_of(timesteps)
    step_here = lax.dynamic_slice_in_dim(step_size, guide_side * guided_count, guided_count, 0)
    next_latent = latent + step_here[None, :, None] * velocity
    return (velocity, next_latent)


def solution(mesh):
    return jax.shard_map(
        body,
        mesh=mesh,
        in_specs=(
            P(("seq", "wgt"), "cfg", None),
            P("cfg", "seq", None, None),
            P("cfg", "seq", None),
            P("cfg", "seq"),
            P(),
            P("cfg", None, None, None),
            P(),
            P(None, "seq", "wgt"),
            P(None, "seq", "wgt"),
            P("wgt", "seq"),
            P("seq", "wgt"),
            P("wgt", "seq"),
            P(),
        ),
        out_specs=(P(("seq", "wgt"), "cfg", None), P(("seq", "wgt"), "cfg", None)),
        check_vma=False,
    )
```

```python
import jax
import jax.numpy as jnp
from jax import lax
from jax.experimental import pallas as pl
from jax.experimental.pallas import tpu as pltpu
from jax.sharding import PartitionSpec as P

STEPS = 28


guidance_scale = 3.5
flow_shift = 3.0
eps_norm = 1e-06
masked_score = -1e30


def from_partner(value, axis, bit):
    mask = 2**bit
    pairs = [(source, source ^ mask) for source in range(lax.axis_size(axis))]
    return lax.ppermute(value, axis, pairs)


def layer_norm(values):
    center = jnp.mean(values, axis=-1, keepdims=True)
    centred = values - center
    spread = jnp.mean(centred * centred, axis=-1, keepdims=True)
    return centred * lax.rsqrt(spread + eps_norm)


def head_norm(values, gain_row):
    power = jnp.mean(values * values, axis=-1, keepdims=True)
    return values * lax.rsqrt(power + eps_norm) * gain_row


def sigma_of(index_row):
    time_left = 1.0 - index_row.astype(jnp.float32) / STEPS
    return flow_shift * time_left / (1.0 + (flow_shift - 1.0) * time_left)


def group_sum(partial, groups):
    swapped = lax.all_to_all(partial, "wgt", 0, 0, tiled=True)
    rows = swapped.shape[0] // groups
    return jnp.sum(swapped.reshape(groups, rows, -1).astype(jnp.float32), axis=0)


def make_attention(heads, head_size, text_at, text_here):
    scale = head_size ** (-0.5)

    def kernel(q_ref, kv_ref, mask_ref, o_ref):
        requests, tokens, cols = q_ref.shape
        blocks = kv_ref.shape[0]
        lane = lax.broadcasted_iota(jnp.int32, (1, cols), 1)
        k_txt = kv_ref[:, text_at : text_at + text_here, :].reshape(blocks * text_here, cols)
        v_txt = kv_ref[:, text_at + text_here : text_at + 2 * text_here, :].reshape(
            blocks * text_here, cols
        )
        dims = (((1,), (1,)), ((), ()))
        for r in range(requests):
            q = q_ref[r].astype(jnp.float32)
            k_img = kv_ref[:, 2 * tokens * r : 2 * tokens * r + tokens, :].reshape(
                blocks * tokens, cols
            )
            v_img = kv_ref[:, 2 * tokens * r + tokens : 2 * tokens * (r + 1), :].reshape(
                blocks * tokens, cols
            )
            allowed = mask_ref[r : r + 1, :] > 0.5
            out = jnp.zeros((tokens, cols), jnp.float32)
            for h in range(heads):
                in_head = (lane >= h * head_size) & (lane < (h + 1) * head_size)
                qh = jnp.where(in_head, q, 0.0).astype(jnp.bfloat16)
                s_img = lax.dot_general(qh, k_img, dims, preferred_element_type=jnp.float32) * scale
                s_txt = lax.dot_general(qh, k_txt, dims, preferred_element_type=jnp.float32) * scale
                s_txt = jnp.where(allowed, s_txt, masked_score)
                top = jnp.maximum(
                    jnp.max(s_img, axis=1, keepdims=True), jnp.max(s_txt, axis=1, keepdims=True)
                )
                p_img = jnp.exp(s_img - top)
                p_txt = jnp.exp(s_txt - top)
                total = jnp.sum(p_img, axis=1, keepdims=True) + jnp.sum(p_txt, axis=1, keepdims=True)
                acc = jnp.dot(
                    p_img.astype(jnp.bfloat16), v_img, preferred_element_type=jnp.float32
                ) + jnp.dot(p_txt.astype(jnp.bfloat16), v_txt, preferred_element_type=jnp.float32)
                out = jnp.where(in_head, acc / total, out)
            o_ref[r] = out.astype(o_ref.dtype)

    def run(q, kv, mask):
        return pl.pallas_call(
            kernel,
            out_shape=jax.ShapeDtypeStruct(q.shape, jnp.bfloat16),
            in_specs=[pl.BlockSpec(memory_space=pltpu.VMEM)] * 3,
            out_specs=pl.BlockSpec(memory_space=pltpu.VMEM),
        )(q, kv, mask)

    return run


def body(
    latent,
    img_hidden,
    txt_hidden,
    segments,
    timesteps,
    modulation,
    qk_gain,
    qkv_weight,
    text_weight,
    out_weight,
    expand_weight,
    contract_weight,
    final_weight,
):
    tokens_here = img_hidden.shape[1]
    requests = img_hidden.shape[2]
    feat_width = img_hidden.shape[3]
    head_size = qk_gain.shape[1]
    local_cols = qkv_weight.shape[2]
    heads_here = local_cols // head_size
    text_here = txt_hidden.shape[1]
    seq_size = lax.axis_size("seq")
    wgt_size = lax.axis_size("wgt")
    modulate = modulation[0]
    hidden = img_hidden[0].astype(jnp.float32)
    image_normed = (layer_norm(hidden) * (1.0 + modulate[:, 1]) + modulate[:, 0]).astype(
        jnp.bfloat16
    )
    row_count = tokens_here * requests
    token_rows = image_normed.reshape(row_count, feat_width)
    segment_row = segments[0]
    one_hot = (segment_row[:, None] == jnp.arange(requests, dtype=jnp.int32)[None, :]).astype(
        jnp.float32
    )
    text_mod = jnp.einsum("tr,rkd->tkd", one_hot, modulate[:, 3:5], precision=lax.Precision.HIGHEST)
    text_normed = (
        layer_norm(txt_hidden[0].astype(jnp.float32)) * (1.0 + text_mod[:, 1]) + text_mod[:, 0]
    ).astype(jnp.bfloat16)
    block_rows = qkv_weight.shape[1]
    padded_rows = block_rows + (-block_rows) % 8
    kinds = qkv_weight.shape[0] + text_weight.shape[0]
    all_weights = jnp.transpose(
        jnp.concatenate([qkv_weight, text_weight], axis=0), (1, 0, 2)
    ).reshape(block_rows, kinds * local_cols)
    all_weights = jnp.pad(all_weights, ((0, padded_rows - block_rows), (0, 0)))
    piece = lax.all_gather(all_weights, "seq", axis=0, tiled=False)
    mlp_local = jnp.pad(
        jnp.stack([expand_weight, contract_weight.T], axis=0),
        ((0, 0), (0, padded_rows - block_rows), (0, 0)),
    )
    mlp_full = lax.all_gather(mlp_local, "seq", axis=0, tiled=False)
    out_full = lax.all_gather(out_weight, "seq", axis=1, tiled=True)
    both_rows = jnp.concatenate([token_rows, text_normed], axis=0)
    both_count = both_rows.shape[0]
    both_cols = jnp.pad(
        both_rows.T.reshape(seq_size, block_rows, both_count),
        ((0, 0), (0, padded_rows - block_rows), (0, 0)),
    )
    both_term = jnp.einsum(
        "sdr,sdn->rn", both_cols, piece, preferred_element_type=jnp.float32
    ).reshape(both_count, kinds, local_cols)
    image_term = both_term[:row_count]
    text_term = both_term[row_count:]
    queries = head_norm(
        image_term[:, 0].reshape(tokens_here, requests, heads_here, head_size), qk_gain[0]
    ).astype(jnp.bfloat16)
    keys_img = head_norm(
        image_term[:, 1].reshape(tokens_here, requests, heads_here, head_size), qk_gain[1]
    ).astype(jnp.bfloat16)
    values_img = image_term[:, 2].reshape(tokens_here, requests, local_cols).astype(jnp.bfloat16)
    keys_txt = head_norm(
        text_term[:, 3].reshape(text_here, heads_here, head_size), qk_gain[1]
    ).astype(jnp.bfloat16)
    values_txt = text_term[:, 4].astype(jnp.bfloat16)
    image_pair = jnp.transpose(
        jnp.stack([keys_img.reshape(tokens_here, requests, local_cols), values_img], axis=0),
        (2, 0, 1, 3),
    ).reshape(requests * 2 * tokens_here, local_cols)
    text_pair = jnp.stack([keys_txt.reshape(text_here, local_cols), values_txt], axis=0).reshape(
        2 * text_here, local_cols
    )
    lanes = local_cols + (-local_cols) % 128
    image_pair = jnp.pad(image_pair, ((0, 0), (0, lanes - local_cols)))
    text_pair = jnp.pad(text_pair, ((0, 0), (0, lanes - local_cols)))
    owner_row = jnp.pad(
        segment_row.astype(jnp.float32).astype(jnp.bfloat16), (0, lanes - text_here)
    )[None, :]
    image_len = requests * 2 * tokens_here
    owner_at = image_len + 2 * text_here
    pad_rows = (-(owner_at + 1)) % 16
    shared = jnp.concatenate(
        [image_pair, text_pair, owner_row, jnp.zeros((pad_rows, lanes), jnp.bfloat16)], axis=0
    )
    shared_piece = lax.all_gather(shared, "seq", axis=0, tiled=False)
    owner_piece = shared_piece[:, owner_at, :text_here].reshape(-1)
    request_ids = jnp.arange(requests, dtype=jnp.float32)
    text_mask = (owner_piece.astype(jnp.float32)[None, :] == request_ids[:, None]).astype(
        jnp.float32
    )
    query_block = jnp.pad(
        jnp.transpose(queries.reshape(tokens_here, requests, local_cols), (1, 0, 2)),
        ((0, 0), (0, 0), (0, lanes - local_cols)),
    )
    attend = make_attention(heads_here, head_size, image_len, text_here)
    attended = attend(query_block, shared_piece, text_mask)
    attended = jnp.transpose(attended[:, :, :local_cols], (1, 0, 2)).reshape(row_count, local_cols)
    share_rows = row_count // wgt_size
    mixed = group_sum(
        jnp.dot(attended, out_full, preferred_element_type=jnp.float32).astype(jnp.bfloat16),
        wgt_size,
    )
    tokens_out = share_rows // requests
    row_place = lax.axis_index("wgt") * share_rows
    base_rows = lax.dynamic_slice_in_dim(
        hidden.reshape(row_count, feat_width), row_place, share_rows, 0
    )
    residual = base_rows.reshape(tokens_out, requests, feat_width) + modulate[:, 2] * mixed.reshape(
        tokens_out, requests, feat_width
    )
    branch_in = (layer_norm(residual) * (1.0 + modulate[:, 6]) + modulate[:, 5]).astype(
        jnp.bfloat16
    )
    branch_rows = lax.all_to_all(
        jnp.broadcast_to(
            branch_in.reshape(1, share_rows, feat_width), (wgt_size, share_rows, feat_width)
        ),
        "wgt",
        0,
        0,
        tiled=True,
    ).reshape(row_count, feat_width)
    padded_rows_in = jnp.pad(
        branch_rows.reshape(row_count, seq_size, block_rows),
        ((0, 0), (0, 0), (0, padded_rows - block_rows)),
    )
    expanded = jnp.einsum(
        "rsd,sdf->rf", padded_rows_in, mlp_full[:, 0], preferred_element_type=jnp.float32
    )
    expanded = jax.nn.gelu(expanded, approximate=True).astype(jnp.bfloat16)
    contract_rows = mlp_full[:, 1].reshape(seq_size * padded_rows, -1)
    contracted = lax.dot_general(
        expanded, contract_rows, (((1,), (1,)), ((), ())), preferred_element_type=jnp.float32
    ).astype(jnp.bfloat16)
    branch = group_sum(contracted, wgt_size)
    branch = branch.reshape(share_rows, seq_size, padded_rows)[:, :, :block_rows].reshape(
        share_rows, feat_width
    )
    second = residual + modulate[:, 7] * branch.reshape(tokens_out, requests, feat_width)
    final_in = (layer_norm(second) * (1.0 + modulate[:, 9]) + modulate[:, 8]).astype(jnp.bfloat16)
    own_velocity = jnp.dot(
        final_in.reshape(share_rows, feat_width), final_weight, preferred_element_type=jnp.float32
    ).reshape(tokens_out, requests, -1)
    guide_side = lax.axis_index("cfg")
    guided_count = latent.shape[1]
    kept_rows = lax.dynamic_slice_in_dim(own_velocity, guide_side * guided_count, guided_count, 1)
    sent_rows = lax.dynamic_slice_in_dim(
        own_velocity, (1 - guide_side) * guided_count, guided_count, 1
    )
    partner_velocity = from_partner(sent_rows, "cfg", 0)
    is_first = guide_side == 0
    conditional = jnp.where(is_first, kept_rows, partner_velocity)
    unconditional = jnp.where(is_first, partner_velocity, kept_rows)
    velocity = unconditional + guidance_scale * (conditional - unconditional)
    step_size = sigma_of(timesteps + 1) - sigma_of(timesteps)
    step_here = lax.dynamic_slice_in_dim(step_size, guide_side * guided_count, guided_count, 0)
    next_latent = latent + step_here[None, :, None] * velocity
    return (velocity, next_latent)


def solution(mesh):
    return jax.shard_map(
        body,
        mesh=mesh,
        in_specs=(
            P(("seq", "wgt"), "cfg", None),
            P("cfg", "seq", None, None),
            P("cfg", "seq", None),
            P("cfg", "seq"),
            P(),
            P("cfg", None, None, None),
            P(),
            P(None, "seq", "wgt"),
            P(None, "seq", "wgt"),
            P("wgt", "seq"),
            P("seq", "wgt"),
            P("wgt", "seq"),
            P(),
        ),
        out_specs=(P(("seq", "wgt"), "cfg", None), P(("seq", "wgt"), "cfg", None)),
        check_vma=False,
    )
```

```python
import jax
import jax.numpy as jnp
from jax import lax
from jax.experimental import pallas as pl
from jax.experimental.pallas import tpu as pltpu
from jax.sharding import PartitionSpec as P

STEPS = 28


guidance_scale = 3.5
flow_shift = 3.0
eps_norm = 1e-06
masked_score = -1e30


def from_partner(value, axis, bit):
    mask = 2**bit
    pairs = [(source, source ^ mask) for source in range(lax.axis_size(axis))]
    return lax.ppermute(value, axis, pairs)


def layer_norm(values):
    center = jnp.mean(values, axis=-1, keepdims=True)
    centred = values - center
    spread = jnp.mean(centred * centred, axis=-1, keepdims=True)
    return centred * lax.rsqrt(spread + eps_norm)


def head_norm(values, gain_row):
    power = jnp.mean(values * values, axis=-1, keepdims=True)
    return values * lax.rsqrt(power + eps_norm) * gain_row


def sigma_of(index_row):
    time_left = 1.0 - index_row.astype(jnp.float32) / STEPS
    return flow_shift * time_left / (1.0 + (flow_shift - 1.0) * time_left)


def group_sum(partial, groups):
    swapped = lax.all_to_all(partial, "wgt", 0, 0, tiled=True)
    rows = swapped.shape[0] // groups
    return jnp.sum(swapped.reshape(groups, rows, -1).astype(jnp.float32), axis=0)


def make_attention(heads, head_size, text_at, text_here):
    scale = head_size ** (-0.5)

    def kernel(q_ref, kv_ref, mask_ref, o_ref):
        requests, tokens, cols = q_ref.shape
        blocks = kv_ref.shape[0]
        lane = lax.broadcasted_iota(jnp.int32, (1, cols), 1)
        k_txt = kv_ref[:, text_at : text_at + text_here, :].reshape(blocks * text_here, cols)
        v_txt = kv_ref[:, text_at + text_here : text_at + 2 * text_here, :].reshape(
            blocks * text_here, cols
        )
        dims = (((1,), (1,)), ((), ()))
        for r in range(requests):
            q = q_ref[r].astype(jnp.float32)
            k_img = kv_ref[:, 2 * tokens * r : 2 * tokens * r + tokens, :].reshape(
                blocks * tokens, cols
            )
            v_img = kv_ref[:, 2 * tokens * r + tokens : 2 * tokens * (r + 1), :].reshape(
                blocks * tokens, cols
            )
            allowed = mask_ref[r : r + 1, :] > 0.5
            out = jnp.zeros((tokens, cols), jnp.float32)
            for h in range(heads):
                in_head = (lane >= h * head_size) & (lane < (h + 1) * head_size)
                qh = jnp.where(in_head, q, 0.0).astype(jnp.bfloat16)
                s_img = lax.dot_general(qh, k_img, dims, preferred_element_type=jnp.float32) * scale
                s_txt = lax.dot_general(qh, k_txt, dims, preferred_element_type=jnp.float32) * scale
                s_txt = jnp.where(allowed, s_txt, masked_score)
                top = jnp.maximum(
                    jnp.max(s_img, axis=1, keepdims=True), jnp.max(s_txt, axis=1, keepdims=True)
                )
                p_img = jnp.exp(s_img - top)
                p_txt = jnp.exp(s_txt - top)
                total = jnp.sum(p_img, axis=1, keepdims=True) + jnp.sum(p_txt, axis=1, keepdims=True)
                acc = jnp.dot(
                    p_img.astype(jnp.bfloat16), v_img, preferred_element_type=jnp.float32
                ) + jnp.dot(p_txt.astype(jnp.bfloat16), v_txt, preferred_element_type=jnp.float32)
                out = jnp.where(in_head, acc / total, out)
            o_ref[r] = out.astype(o_ref.dtype)

    def run(q, kv, mask):
        return pl.pallas_call(
            kernel,
            out_shape=jax.ShapeDtypeStruct(q.shape, jnp.bfloat16),
            in_specs=[pl.BlockSpec(memory_space=pltpu.VMEM)] * 3,
            out_specs=pl.BlockSpec(memory_space=pltpu.VMEM),
        )(q, kv, mask)

    return run


def body(
    latent,
    img_hidden,
    txt_hidden,
    segments,
    timesteps,
    modulation,
    qk_gain,
    qkv_weight,
    text_weight,
    out_weight,
    expand_weight,
    contract_weight,
    final_weight,
):
    tokens_here = img_hidden.shape[1]
    requests = img_hidden.shape[2]
    feat_width = img_hidden.shape[3]
    head_size = qk_gain.shape[1]
    local_cols = qkv_weight.shape[2]
    heads_here = local_cols // head_size
    text_here = txt_hidden.shape[1]
    seq_size = lax.axis_size("seq")
    wgt_size = lax.axis_size("wgt")
    modulate = modulation[0]
    hidden = img_hidden[0].astype(jnp.float32)
    image_normed = (layer_norm(hidden) * (1.0 + modulate[:, 1]) + modulate[:, 0]).astype(
        jnp.bfloat16
    )
    row_count = tokens_here * requests
    token_rows = image_normed.reshape(row_count, feat_width)
    segment_row = segments[0]
    one_hot = (segment_row[:, None] == jnp.arange(requests, dtype=jnp.int32)[None, :]).astype(
        jnp.float32
    )
    text_mod = jnp.einsum("tr,rkd->tkd", one_hot, modulate[:, 3:5], precision=lax.Precision.HIGHEST)
    text_normed = (
        layer_norm(txt_hidden[0].astype(jnp.float32)) * (1.0 + text_mod[:, 1]) + text_mod[:, 0]
    ).astype(jnp.bfloat16)
    block_rows = qkv_weight.shape[1]
    padded_rows = block_rows + (-block_rows) % 8
    kinds = qkv_weight.shape[0] + text_weight.shape[0]
    all_weights = jnp.transpose(
        jnp.concatenate([qkv_weight, text_weight], axis=0), (1, 0, 2)
    ).reshape(block_rows, kinds * local_cols)
    all_weights = jnp.pad(all_weights, ((0, padded_rows - block_rows), (0, 0)))
    piece = lax.all_gather(all_weights, "seq", axis=0, tiled=False)
    mlp_local = jnp.pad(
        jnp.stack([expand_weight, contract_weight.T], axis=0),
        ((0, 0), (0, padded_rows - block_rows), (0, 0)),
    )
    mlp_full = lax.all_gather(mlp_local, "seq", axis=1, tiled=False)
    out_full = lax.all_gather(out_weight, "seq", axis=1, tiled=True)
    both_rows = jnp.concatenate([token_rows, text_normed], axis=0)
    both_count = both_rows.shape[0]
    both_cols = jnp.pad(
        both_rows.T.reshape(seq_size, block_rows, both_count),
        ((0, 0), (0, padded_rows - block_rows), (0, 0)),
    )
    both_term = jnp.einsum(
        "sdr,sdn->rn", both_cols, piece, preferred_element_type=jnp.float32
    ).reshape(both_count, kinds, local_cols)
    image_term = both_term[:row_count]
    text_term = both_term[row_count:]
    queries = head_norm(
        image_term[:, 0].reshape(tokens_here, requests, heads_here, head_size), qk_gain[0]
    ).astype(jnp.bfloat16)
    keys_img = head_norm(
        image_term[:, 1].reshape(tokens_here, requests, heads_here, head_size), qk_gain[1]
    ).astype(jnp.bfloat16)
    values_img = image_term[:, 2].reshape(tokens_here, requests, local_cols).astype(jnp.bfloat16)
    keys_txt = head_norm(
        text_term[:, 3].reshape(text_here, heads_here, head_size), qk_gain[1]
    ).astype(jnp.bfloat16)
    values_txt = text_term[:, 4].astype(jnp.bfloat16)
    image_pair = jnp.transpose(
        jnp.stack([keys_img.reshape(tokens_here, requests, local_cols), values_img], axis=0),
        (2, 0, 1, 3),
    ).reshape(requests * 2 * tokens_here, local_cols)
    text_pair = jnp.stack([keys_txt.reshape(text_here, local_cols), values_txt], axis=0).reshape(
        2 * text_here, local_cols
    )
    lanes = local_cols + (-local_cols) % 128
    image_pair = jnp.pad(image_pair, ((0, 0), (0, lanes - local_cols)))
    text_pair = jnp.pad(text_pair, ((0, 0), (0, lanes - local_cols)))
    owner_row = jnp.pad(
        segment_row.astype(jnp.float32).astype(jnp.bfloat16), (0, lanes - text_here)
    )[None, :]
    image_len = requests * 2 * tokens_here
    owner_at = image_len + 2 * text_here
    pad_rows = (-(owner_at + 1)) % 16
    shared = jnp.concatenate(
        [image_pair, text_pair, owner_row, jnp.zeros((pad_rows, lanes), jnp.bfloat16)], axis=0
    )
    shared_piece = lax.all_gather(shared, "seq", axis=0, tiled=False)
    owner_piece = shared_piece[:, owner_at, :text_here].reshape(-1)
    request_ids = jnp.arange(requests, dtype=jnp.float32)
    text_mask = (owner_piece.astype(jnp.float32)[None, :] == request_ids[:, None]).astype(
        jnp.float32
    )
    query_block = jnp.pad(
        jnp.transpose(queries.reshape(tokens_here, requests, local_cols), (1, 0, 2)),
        ((0, 0), (0, 0), (0, lanes - local_cols)),
    )
    attend = make_attention(heads_here, head_size, image_len, text_here)
    attended = attend(query_block, shared_piece, text_mask)
    attended = jnp.transpose(attended[:, :, :local_cols], (1, 0, 2)).reshape(row_count, local_cols)
    share_rows = row_count // wgt_size
    mixed = group_sum(
        jnp.dot(attended, out_full, preferred_element_type=jnp.float32).astype(jnp.bfloat16),
        wgt_size,
    )
    tokens_out = share_rows // requests
    row_place = lax.axis_index("wgt") * share_rows
    base_rows = lax.dynamic_slice_in_dim(
        hidden.reshape(row_count, feat_width), row_place, share_rows, 0
    )
    residual = base_rows.reshape(tokens_out, requests, feat_width) + modulate[:, 2] * mixed.reshape(
        tokens_out, requests, feat_width
    )
    branch_in = (layer_norm(residual) * (1.0 + modulate[:, 6]) + modulate[:, 5]).astype(
        jnp.bfloat16
    )
    branch_rows = lax.all_to_all(
        jnp.broadcast_to(
            branch_in.reshape(1, share_rows, feat_width), (wgt_size, share_rows, feat_width)
        ),
        "wgt",
        0,
        0,
        tiled=True,
    ).reshape(row_count, feat_width)
    padded_rows_in = jnp.pad(
        branch_rows.reshape(row_count, seq_size, block_rows),
        ((0, 0), (0, 0), (0, padded_rows - block_rows)),
    )
    expanded = jnp.einsum(
        "rsd,sdf->rf", padded_rows_in, mlp_full[0], preferred_element_type=jnp.float32
    )
    expanded = jax.nn.gelu(expanded, approximate=True).astype(jnp.bfloat16)
    contract_rows = mlp_full[1].reshape(seq_size * padded_rows, -1)
    contracted = lax.dot_general(
        expanded, contract_rows, (((1,), (1,)), ((), ())), preferred_element_type=jnp.float32
    ).astype(jnp.bfloat16)
    branch = group_sum(contracted, wgt_size)
    branch = branch.reshape(share_rows, seq_size, padded_rows)[:, :, :block_rows].reshape(
        share_rows, feat_width
    )
    second = residual + modulate[:, 7] * branch.reshape(tokens_out, requests, feat_width)
    final_in = (layer_norm(second) * (1.0 + modulate[:, 9]) + modulate[:, 8]).astype(jnp.bfloat16)
    own_velocity = jnp.dot(
        final_in.reshape(share_rows, feat_width), final_weight, preferred_element_type=jnp.float32
    ).reshape(tokens_out, requests, -1)
    guide_side = lax.axis_index("cfg")
    guided_count = latent.shape[1]
    kept_rows = lax.dynamic_slice_in_dim(own_velocity, guide_side * guided_count, guided_count, 1)
    sent_rows = lax.dynamic_slice_in_dim(
        own_velocity, (1 - guide_side) * guided_count, guided_count, 1
    )
    partner_velocity = from_partner(sent_rows, "cfg", 0)
    is_first = guide_side == 0
    conditional = jnp.where(is_first, kept_rows, partner_velocity)
    unconditional = jnp.where(is_first, partner_velocity, kept_rows)
    velocity = unconditional + guidance_scale * (conditional - unconditional)
    step_size = sigma_of(timesteps + 1) - sigma_of(timesteps)
    step_here = lax.dynamic_slice_in_dim(step_size, guide_side * guided_count, guided_count, 0)
    next_latent = latent + step_here[None, :, None] * velocity
    return (velocity, next_latent)


def solution(mesh):
    return jax.shard_map(
        body,
        mesh=mesh,
        in_specs=(
            P(("seq", "wgt"), "cfg", None),
            P("cfg", "seq", None, None),
            P("cfg", "seq", None),
            P("cfg", "seq"),
            P(),
            P("cfg", None, None, None),
            P(),
            P(None, "seq", "wgt"),
            P(None, "seq", "wgt"),
            P("wgt", "seq"),
            P("seq", "wgt"),
            P("wgt", "seq"),
            P(),
        ),
        out_specs=(P(("seq", "wgt"), "cfg", None), P(("seq", "wgt"), "cfg", None)),
        check_vma=False,
    )
```

```python
import jax
import jax.numpy as jnp
from jax import lax
from jax.experimental import pallas as pl
from jax.experimental.pallas import tpu as pltpu
from jax.sharding import PartitionSpec as P

STEPS = 28


guidance_scale = 3.5
flow_shift = 3.0
eps_norm = 1e-06
masked_score = -1e30


def from_partner(value, axis, bit):
    mask = 2**bit
    pairs = [(source, source ^ mask) for source in range(lax.axis_size(axis))]
    return lax.ppermute(value, axis, pairs)


def layer_norm(values):
    center = jnp.mean(values, axis=-1, keepdims=True)
    centred = values - center
    spread = jnp.mean(centred * centred, axis=-1, keepdims=True)
    return centred * lax.rsqrt(spread + eps_norm)


def head_norm(values, gain_row):
    power = jnp.mean(values * values, axis=-1, keepdims=True)
    return values * lax.rsqrt(power + eps_norm) * gain_row


def sigma_of(index_row):
    time_left = 1.0 - index_row.astype(jnp.float32) / STEPS
    return flow_shift * time_left / (1.0 + (flow_shift - 1.0) * time_left)


def group_sum(partial, groups):
    swapped = lax.all_to_all(partial, "wgt", 0, 0, tiled=True)
    rows = swapped.shape[0] // groups
    return jnp.sum(swapped.reshape(groups, rows, -1).astype(jnp.float32), axis=0)


def make_attention(heads, head_size, text_at, text_here):
    scale = head_size ** (-0.5)

    def kernel(q_ref, kv_ref, mask_ref, o_ref):
        requests, tokens, cols = q_ref.shape
        blocks = kv_ref.shape[0]
        lane = lax.broadcasted_iota(jnp.int32, (1, cols), 1)
        k_txt = kv_ref[:, text_at : text_at + text_here, :].reshape(blocks * text_here, cols)
        v_txt = kv_ref[:, text_at + text_here : text_at + 2 * text_here, :].reshape(
            blocks * text_here, cols
        )
        dims = (((1,), (1,)), ((), ()))
        for r in range(requests):
            q = q_ref[r].astype(jnp.float32)
            k_img = kv_ref[:, 2 * tokens * r : 2 * tokens * r + tokens, :].reshape(
                blocks * tokens, cols
            )
            v_img = kv_ref[:, 2 * tokens * r + tokens : 2 * tokens * (r + 1), :].reshape(
                blocks * tokens, cols
            )
            allowed = mask_ref[r : r + 1, :] > 0.5
            out = jnp.zeros((tokens, cols), jnp.float32)
            for h in range(heads):
                in_head = (lane >= h * head_size) & (lane < (h + 1) * head_size)
                qh = jnp.where(in_head, q, 0.0).astype(jnp.bfloat16)
                s_img = lax.dot_general(qh, k_img, dims, preferred_element_type=jnp.float32) * scale
                s_txt = lax.dot_general(qh, k_txt, dims, preferred_element_type=jnp.float32) * scale
                s_txt = jnp.where(allowed, s_txt, masked_score)
                top = jnp.maximum(
                    jnp.max(s_img, axis=1, keepdims=True), jnp.max(s_txt, axis=1, keepdims=True)
                )
                p_img = jnp.exp(s_img - top)
                p_txt = jnp.exp(s_txt - top)
                total = jnp.sum(p_img, axis=1, keepdims=True) + jnp.sum(p_txt, axis=1, keepdims=True)
                acc = jnp.dot(
                    p_img.astype(jnp.bfloat16), v_img, preferred_element_type=jnp.float32
                ) + jnp.dot(p_txt.astype(jnp.bfloat16), v_txt, preferred_element_type=jnp.float32)
                out = jnp.where(in_head, acc / total, out)
            o_ref[r] = out.astype(o_ref.dtype)

    def run(q, kv, mask):
        return pl.pallas_call(
            kernel,
            out_shape=jax.ShapeDtypeStruct(q.shape, jnp.bfloat16),
            in_specs=[pl.BlockSpec(memory_space=pltpu.VMEM)] * 3,
            out_specs=pl.BlockSpec(memory_space=pltpu.VMEM),
        )(q, kv, mask)

    return run


def mlp_kernel(x_ref, w_ref, o_ref):
    blocks, _, rows, units = w_ref.shape
    expand = w_ref[:, 0].reshape(blocks * rows, units)
    grown = jnp.dot(x_ref[...], expand, preferred_element_type=jnp.float32)
    grown = jax.nn.gelu(grown, approximate=True).astype(jnp.bfloat16)
    contract = w_ref[:, 1].reshape(blocks * rows, units)
    o_ref[...] = lax.dot_general(
        grown, contract, (((1,), (1,)), ((), ())), preferred_element_type=jnp.float32
    ).astype(o_ref.dtype)


def run_mlp(rows_in, weights):
    blocks, _, rows, _ = weights.shape
    return pl.pallas_call(
        mlp_kernel,
        out_shape=jax.ShapeDtypeStruct((rows_in.shape[0], blocks * rows), jnp.bfloat16),
        in_specs=[pl.BlockSpec(memory_space=pltpu.VMEM)] * 2,
        out_specs=pl.BlockSpec(memory_space=pltpu.VMEM),
    )(rows_in, weights)


def body(
    latent,
    img_hidden,
    txt_hidden,
    segments,
    timesteps,
    modulation,
    qk_gain,
    qkv_weight,
    text_weight,
    out_weight,
    expand_weight,
    contract_weight,
    final_weight,
):
    tokens_here = img_hidden.shape[1]
    requests = img_hidden.shape[2]
    feat_width = img_hidden.shape[3]
    head_size = qk_gain.shape[1]
    local_cols = qkv_weight.shape[2]
    heads_here = local_cols // head_size
    text_here = txt_hidden.shape[1]
    seq_size = lax.axis_size("seq")
    wgt_size = lax.axis_size("wgt")
    modulate = modulation[0]
    hidden = img_hidden[0].astype(jnp.float32)
    image_normed = (layer_norm(hidden) * (1.0 + modulate[:, 1]) + modulate[:, 0]).astype(
        jnp.bfloat16
    )
    row_count = tokens_here * requests
    token_rows = image_normed.reshape(row_count, feat_width)
    segment_row = segments[0]
    one_hot = (segment_row[:, None] == jnp.arange(requests, dtype=jnp.int32)[None, :]).astype(
        jnp.float32
    )
    text_mod = jnp.einsum("tr,rkd->tkd", one_hot, modulate[:, 3:5], precision=lax.Precision.HIGHEST)
    text_normed = (
        layer_norm(txt_hidden[0].astype(jnp.float32)) * (1.0 + text_mod[:, 1]) + text_mod[:, 0]
    ).astype(jnp.bfloat16)
    block_rows = qkv_weight.shape[1]
    padded_rows = block_rows + (-block_rows) % 8
    kinds = qkv_weight.shape[0] + text_weight.shape[0]
    all_weights = jnp.transpose(
        jnp.concatenate([qkv_weight, text_weight], axis=0), (1, 0, 2)
    ).reshape(block_rows, kinds * local_cols)
    all_weights = jnp.pad(all_weights, ((0, padded_rows - block_rows), (0, 0)))
    piece = lax.all_gather(all_weights, "seq", axis=0, tiled=False)
    mlp_local = jnp.pad(
        jnp.stack([expand_weight, contract_weight.T], axis=0),
        ((0, 0), (0, padded_rows - block_rows), (0, 0)),
    )
    mlp_full = lax.all_gather(mlp_local, "seq", axis=0, tiled=False)
    out_full = lax.all_gather(out_weight, "seq", axis=1, tiled=True)
    both_rows = jnp.concatenate([token_rows, text_normed], axis=0)
    both_count = both_rows.shape[0]
    both_cols = jnp.pad(
        both_rows.T.reshape(seq_size, block_rows, both_count),
        ((0, 0), (0, padded_rows - block_rows), (0, 0)),
    )
    both_term = jnp.einsum(
        "sdr,sdn->rn", both_cols, piece, preferred_element_type=jnp.float32
    ).reshape(both_count, kinds, local_cols)
    image_term = both_term[:row_count]
    text_term = both_term[row_count:]
    queries = head_norm(
        image_term[:, 0].reshape(tokens_here, requests, heads_here, head_size), qk_gain[0]
    ).astype(jnp.bfloat16)
    keys_img = head_norm(
        image_term[:, 1].reshape(tokens_here, requests, heads_here, head_size), qk_gain[1]
    ).astype(jnp.bfloat16)
    values_img = image_term[:, 2].reshape(tokens_here, requests, local_cols).astype(jnp.bfloat16)
    keys_txt = head_norm(
        text_term[:, 3].reshape(text_here, heads_here, head_size), qk_gain[1]
    ).astype(jnp.bfloat16)
    values_txt = text_term[:, 4].astype(jnp.bfloat16)
    image_pair = jnp.transpose(
        jnp.stack([keys_img.reshape(tokens_here, requests, local_cols), values_img], axis=0),
        (2, 0, 1, 3),
    ).reshape(requests * 2 * tokens_here, local_cols)
    text_pair = jnp.stack([keys_txt.reshape(text_here, local_cols), values_txt], axis=0).reshape(
        2 * text_here, local_cols
    )
    lanes = local_cols + (-local_cols) % 128
    image_pair = jnp.pad(image_pair, ((0, 0), (0, lanes - local_cols)))
    text_pair = jnp.pad(text_pair, ((0, 0), (0, lanes - local_cols)))
    owner_row = jnp.pad(
        segment_row.astype(jnp.float32).astype(jnp.bfloat16), (0, lanes - text_here)
    )[None, :]
    image_len = requests * 2 * tokens_here
    owner_at = image_len + 2 * text_here
    pad_rows = (-(owner_at + 1)) % 16
    shared = jnp.concatenate(
        [image_pair, text_pair, owner_row, jnp.zeros((pad_rows, lanes), jnp.bfloat16)], axis=0
    )
    shared_piece = lax.all_gather(shared, "seq", axis=0, tiled=False)
    owner_piece = shared_piece[:, owner_at, :text_here].reshape(-1)
    request_ids = jnp.arange(requests, dtype=jnp.float32)
    text_mask = (owner_piece.astype(jnp.float32)[None, :] == request_ids[:, None]).astype(
        jnp.float32
    )
    query_block = jnp.pad(
        jnp.transpose(queries.reshape(tokens_here, requests, local_cols), (1, 0, 2)),
        ((0, 0), (0, 0), (0, lanes - local_cols)),
    )
    attend = make_attention(heads_here, head_size, image_len, text_here)
    attended = attend(query_block, shared_piece, text_mask)
    attended = jnp.transpose(attended[:, :, :local_cols], (1, 0, 2)).reshape(row_count, local_cols)
    share_rows = row_count // wgt_size
    mixed = group_sum(
        jnp.dot(attended, out_full, preferred_element_type=jnp.float32).astype(jnp.bfloat16),
        wgt_size,
    )
    tokens_out = share_rows // requests
    row_place = lax.axis_index("wgt") * share_rows
    base_rows = lax.dynamic_slice_in_dim(
        hidden.reshape(row_count, feat_width), row_place, share_rows, 0
    )
    residual = base_rows.reshape(tokens_out, requests, feat_width) + modulate[:, 2] * mixed.reshape(
        tokens_out, requests, feat_width
    )
    branch_in = (layer_norm(residual) * (1.0 + modulate[:, 6]) + modulate[:, 5]).astype(
        jnp.bfloat16
    )
    branch_rows = lax.all_to_all(
        jnp.broadcast_to(
            branch_in.reshape(1, share_rows, feat_width), (wgt_size, share_rows, feat_width)
        ),
        "wgt",
        0,
        0,
        tiled=True,
    ).reshape(row_count, feat_width)
    padded_rows_in = jnp.pad(
        branch_rows.reshape(row_count, seq_size, block_rows),
        ((0, 0), (0, 0), (0, padded_rows - block_rows)),
    )
    contracted = run_mlp(padded_rows_in.reshape(row_count, seq_size * padded_rows), mlp_full)
    branch = group_sum(contracted, wgt_size)
    branch = branch.reshape(share_rows, seq_size, padded_rows)[:, :, :block_rows].reshape(
        share_rows, feat_width
    )
    second = residual + modulate[:, 7] * branch.reshape(tokens_out, requests, feat_width)
    final_in = (layer_norm(second) * (1.0 + modulate[:, 9]) + modulate[:, 8]).astype(jnp.bfloat16)
    own_velocity = jnp.dot(
        final_in.reshape(share_rows, feat_width), final_weight, preferred_element_type=jnp.float32
    ).reshape(tokens_out, requests, -1)
    guide_side = lax.axis_index("cfg")
    guided_count = latent.shape[1]
    kept_rows = lax.dynamic_slice_in_dim(own_velocity, guide_side * guided_count, guided_count, 1)
    sent_rows = lax.dynamic_slice_in_dim(
        own_velocity, (1 - guide_side) * guided_count, guided_count, 1
    )
    partner_velocity = from_partner(sent_rows, "cfg", 0)
    is_first = guide_side == 0
    conditional = jnp.where(is_first, kept_rows, partner_velocity)
    unconditional = jnp.where(is_first, partner_velocity, kept_rows)
    velocity = unconditional + guidance_scale * (conditional - unconditional)
    step_size = sigma_of(timesteps + 1) - sigma_of(timesteps)
    step_here = lax.dynamic_slice_in_dim(step_size, guide_side * guided_count, guided_count, 0)
    next_latent = latent + step_here[None, :, None] * velocity
    return (velocity, next_latent)


def solution(mesh):
    return jax.shard_map(
        body,
        mesh=mesh,
        in_specs=(
            P(("seq", "wgt"), "cfg", None),
            P("cfg", "seq", None, None),
            P("cfg", "seq", None),
            P("cfg", "seq"),
            P(),
            P("cfg", None, None, None),
            P(),
            P(None, "seq", "wgt"),
            P(None, "seq", "wgt"),
            P("wgt", "seq"),
            P("seq", "wgt"),
            P("wgt", "seq"),
            P(),
        ),
        out_specs=(P(("seq", "wgt"), "cfg", None), P(("seq", "wgt"), "cfg", None)),
        check_vma=False,
    )
```

```python
import jax
import jax.numpy as jnp
from jax import lax
from jax.experimental import pallas as pl
from jax.experimental.pallas import tpu as pltpu
from jax.sharding import PartitionSpec as P

STEPS = 28


guidance_scale = 3.5
flow_shift = 3.0
eps_norm = 1e-06
masked_score = -1e30


def from_partner(value, axis, bit):
    mask = 2**bit
    pairs = [(source, source ^ mask) for source in range(lax.axis_size(axis))]
    return lax.ppermute(value, axis, pairs)


def layer_norm(values):
    center = jnp.mean(values, axis=-1, keepdims=True)
    centred = values - center
    spread = jnp.mean(centred * centred, axis=-1, keepdims=True)
    return centred * lax.rsqrt(spread + eps_norm)


def head_norm(values, gain_row):
    power = jnp.mean(values * values, axis=-1, keepdims=True)
    return values * lax.rsqrt(power + eps_norm) * gain_row


def sigma_of(index_row):
    time_left = 1.0 - index_row.astype(jnp.float32) / STEPS
    return flow_shift * time_left / (1.0 + (flow_shift - 1.0) * time_left)


def group_sum(partial, groups):
    swapped = lax.all_to_all(partial, "wgt", 0, 0, tiled=True)
    rows = swapped.shape[0] // groups
    return jnp.sum(swapped.reshape(groups, rows, -1).astype(jnp.float32), axis=0)


def make_attention(heads, head_size, text_at, text_here):
    scale = head_size ** (-0.5)

    def kernel(q_ref, kv_ref, mask_ref, o_ref):
        requests, tokens, cols = q_ref.shape
        blocks = kv_ref.shape[0]
        lane = lax.broadcasted_iota(jnp.int32, (1, cols), 1)
        k_txt = kv_ref[:, text_at : text_at + text_here, :].reshape(blocks * text_here, cols)
        v_txt = kv_ref[:, text_at + text_here : text_at + 2 * text_here, :].reshape(
            blocks * text_here, cols
        )
        dims = (((1,), (1,)), ((), ()))
        for r in range(requests):
            q = q_ref[r].astype(jnp.float32)
            k_img = kv_ref[:, 2 * tokens * r : 2 * tokens * r + tokens, :].reshape(
                blocks * tokens, cols
            )
            v_img = kv_ref[:, 2 * tokens * r + tokens : 2 * tokens * (r + 1), :].reshape(
                blocks * tokens, cols
            )
            allowed = mask_ref[r : r + 1, :] > 0.5
            out = jnp.zeros((tokens, cols), jnp.float32)
            for h in range(heads):
                in_head = (lane >= h * head_size) & (lane < (h + 1) * head_size)
                qh = jnp.where(in_head, q, 0.0).astype(jnp.bfloat16)
                s_img = lax.dot_general(qh, k_img, dims, preferred_element_type=jnp.float32) * scale
                s_txt = lax.dot_general(qh, k_txt, dims, preferred_element_type=jnp.float32) * scale
                s_txt = jnp.where(allowed, s_txt, masked_score)
                top = jnp.maximum(
                    jnp.max(s_img, axis=1, keepdims=True), jnp.max(s_txt, axis=1, keepdims=True)
                )
                p_img = jnp.exp(s_img - top)
                p_txt = jnp.exp(s_txt - top)
                total = jnp.sum(p_img, axis=1, keepdims=True) + jnp.sum(p_txt, axis=1, keepdims=True)
                acc = jnp.dot(
                    p_img.astype(jnp.bfloat16), v_img, preferred_element_type=jnp.float32
                ) + jnp.dot(p_txt.astype(jnp.bfloat16), v_txt, preferred_element_type=jnp.float32)
                out = jnp.where(in_head, acc / total, out)
            o_ref[r] = out.astype(o_ref.dtype)

    def run(q, kv, mask):
        return pl.pallas_call(
            kernel,
            out_shape=jax.ShapeDtypeStruct(q.shape, jnp.bfloat16),
            in_specs=[pl.BlockSpec(memory_space=pltpu.VMEM)] * 3,
            out_specs=pl.BlockSpec(memory_space=pltpu.VMEM),
        )(q, kv, mask)

    return run


def mlp_kernel(x_ref, w_hbm, o_ref, expand_buf, contract_buf, sems):
    blocks, rows, units = expand_buf.shape
    expand_copy = pltpu.make_async_copy(w_hbm.at[:, 0], expand_buf, sems.at[0])
    contract_copy = pltpu.make_async_copy(w_hbm.at[:, 1], contract_buf, sems.at[1])
    expand_copy.start()
    contract_copy.start()
    expand_copy.wait()
    expand = expand_buf[...].reshape(blocks * rows, units)
    grown = jnp.dot(x_ref[...], expand, preferred_element_type=jnp.float32)
    grown = jax.nn.gelu(grown, approximate=True).astype(jnp.bfloat16)
    contract_copy.wait()
    contract = contract_buf[...].reshape(blocks * rows, units)
    o_ref[...] = lax.dot_general(
        grown, contract, (((1,), (1,)), ((), ())), preferred_element_type=jnp.float32
    ).astype(o_ref.dtype)


def run_mlp(rows_in, weights):
    blocks, _, rows, units = weights.shape
    return pl.pallas_call(
        mlp_kernel,
        out_shape=jax.ShapeDtypeStruct((rows_in.shape[0], blocks * rows), jnp.bfloat16),
        in_specs=[pl.BlockSpec(memory_space=pltpu.VMEM), pl.BlockSpec(memory_space=pl.ANY)],
        out_specs=pl.BlockSpec(memory_space=pltpu.VMEM),
        scratch_shapes=[
            pltpu.VMEM((blocks, rows, units), weights.dtype),
            pltpu.VMEM((blocks, rows, units), weights.dtype),
            pltpu.SemaphoreType.DMA((2,)),
        ],
    )(rows_in, weights)


def body(
    latent,
    img_hidden,
    txt_hidden,
    segments,
    timesteps,
    modulation,
    qk_gain,
    qkv_weight,
    text_weight,
    out_weight,
    expand_weight,
    contract_weight,
    final_weight,
):
    tokens_here = img_hidden.shape[1]
    requests = img_hidden.shape[2]
    feat_width = img_hidden.shape[3]
    head_size = qk_gain.shape[1]
    local_cols = qkv_weight.shape[2]
    heads_here = local_cols // head_size
    text_here = txt_hidden.shape[1]
    seq_size = lax.axis_size("seq")
    wgt_size = lax.axis_size("wgt")
    modulate = modulation[0]
    hidden = img_hidden[0].astype(jnp.float32)
    image_normed = (layer_norm(hidden) * (1.0 + modulate[:, 1]) + modulate[:, 0]).astype(
        jnp.bfloat16
    )
    row_count = tokens_here * requests
    token_rows = image_normed.reshape(row_count, feat_width)
    segment_row = segments[0]
    one_hot = (segment_row[:, None] == jnp.arange(requests, dtype=jnp.int32)[None, :]).astype(
        jnp.float32
    )
    text_mod = jnp.einsum("tr,rkd->tkd", one_hot, modulate[:, 3:5], precision=lax.Precision.HIGHEST)
    text_normed = (
        layer_norm(txt_hidden[0].astype(jnp.float32)) * (1.0 + text_mod[:, 1]) + text_mod[:, 0]
    ).astype(jnp.bfloat16)
    block_rows = qkv_weight.shape[1]
    padded_rows = block_rows + (-block_rows) % 8
    kinds = qkv_weight.shape[0] + text_weight.shape[0]
    all_weights = jnp.transpose(
        jnp.concatenate([qkv_weight, text_weight], axis=0), (1, 0, 2)
    ).reshape(block_rows, kinds * local_cols)
    all_weights = jnp.pad(all_weights, ((0, padded_rows - block_rows), (0, 0)))
    piece = lax.all_gather(all_weights, "seq", axis=0, tiled=False)
    mlp_local = jnp.pad(
        jnp.stack([expand_weight, contract_weight.T], axis=0),
        ((0, 0), (0, padded_rows - block_rows), (0, 0)),
    )
    mlp_full = lax.all_gather(mlp_local, "seq", axis=0, tiled=False)
    out_full = lax.all_gather(out_weight, "seq", axis=1, tiled=True)
    both_rows = jnp.concatenate([token_rows, text_normed], axis=0)
    both_count = both_rows.shape[0]
    both_cols = jnp.pad(
        both_rows.T.reshape(seq_size, block_rows, both_count),
        ((0, 0), (0, padded_rows - block_rows), (0, 0)),
    )
    both_term = jnp.einsum(
        "sdr,sdn->rn", both_cols, piece, preferred_element_type=jnp.float32
    ).reshape(both_count, kinds, local_cols)
    image_term = both_term[:row_count]
    text_term = both_term[row_count:]
    queries = head_norm(
        image_term[:, 0].reshape(tokens_here, requests, heads_here, head_size), qk_gain[0]
    ).astype(jnp.bfloat16)
    keys_img = head_norm(
        image_term[:, 1].reshape(tokens_here, requests, heads_here, head_size), qk_gain[1]
    ).astype(jnp.bfloat16)
    values_img = image_term[:, 2].reshape(tokens_here, requests, local_cols).astype(jnp.bfloat16)
    keys_txt = head_norm(
        text_term[:, 3].reshape(text_here, heads_here, head_size), qk_gain[1]
    ).astype(jnp.bfloat16)
    values_txt = text_term[:, 4].astype(jnp.bfloat16)
    image_pair = jnp.transpose(
        jnp.stack([keys_img.reshape(tokens_here, requests, local_cols), values_img], axis=0),
        (2, 0, 1, 3),
    ).reshape(requests * 2 * tokens_here, local_cols)
    text_pair = jnp.stack([keys_txt.reshape(text_here, local_cols), values_txt], axis=0).reshape(
        2 * text_here, local_cols
    )
    lanes = local_cols + (-local_cols) % 128
    image_pair = jnp.pad(image_pair, ((0, 0), (0, lanes - local_cols)))
    text_pair = jnp.pad(text_pair, ((0, 0), (0, lanes - local_cols)))
    owner_row = jnp.pad(
        segment_row.astype(jnp.float32).astype(jnp.bfloat16), (0, lanes - text_here)
    )[None, :]
    image_len = requests * 2 * tokens_here
    owner_at = image_len + 2 * text_here
    pad_rows = (-(owner_at + 1)) % 16
    shared = jnp.concatenate(
        [image_pair, text_pair, owner_row, jnp.zeros((pad_rows, lanes), jnp.bfloat16)], axis=0
    )
    shared_piece = lax.all_gather(shared, "seq", axis=0, tiled=False)
    owner_piece = shared_piece[:, owner_at, :text_here].reshape(-1)
    request_ids = jnp.arange(requests, dtype=jnp.float32)
    text_mask = (owner_piece.astype(jnp.float32)[None, :] == request_ids[:, None]).astype(
        jnp.float32
    )
    query_block = jnp.pad(
        jnp.transpose(queries.reshape(tokens_here, requests, local_cols), (1, 0, 2)),
        ((0, 0), (0, 0), (0, lanes - local_cols)),
    )
    attend = make_attention(heads_here, head_size, image_len, text_here)
    attended = attend(query_block, shared_piece, text_mask)
    attended = jnp.transpose(attended[:, :, :local_cols], (1, 0, 2)).reshape(row_count, local_cols)
    share_rows = row_count // wgt_size
    mixed = group_sum(
        jnp.dot(attended, out_full, preferred_element_type=jnp.float32).astype(jnp.bfloat16),
        wgt_size,
    )
    tokens_out = share_rows // requests
    row_place = lax.axis_index("wgt") * share_rows
    base_rows = lax.dynamic_slice_in_dim(
        hidden.reshape(row_count, feat_width), row_place, share_rows, 0
    )
    residual = base_rows.reshape(tokens_out, requests, feat_width) + modulate[:, 2] * mixed.reshape(
        tokens_out, requests, feat_width
    )
    branch_in = (layer_norm(residual) * (1.0 + modulate[:, 6]) + modulate[:, 5]).astype(
        jnp.bfloat16
    )
    branch_rows = lax.all_to_all(
        jnp.broadcast_to(
            branch_in.reshape(1, share_rows, feat_width), (wgt_size, share_rows, feat_width)
        ),
        "wgt",
        0,
        0,
        tiled=True,
    ).reshape(row_count, feat_width)
    padded_rows_in = jnp.pad(
        branch_rows.reshape(row_count, seq_size, block_rows),
        ((0, 0), (0, 0), (0, padded_rows - block_rows)),
    )
    contracted = run_mlp(padded_rows_in.reshape(row_count, seq_size * padded_rows), mlp_full)
    branch = group_sum(contracted, wgt_size)
    branch = branch.reshape(share_rows, seq_size, padded_rows)[:, :, :block_rows].reshape(
        share_rows, feat_width
    )
    second = residual + modulate[:, 7] * branch.reshape(tokens_out, requests, feat_width)
    final_in = (layer_norm(second) * (1.0 + modulate[:, 9]) + modulate[:, 8]).astype(jnp.bfloat16)
    own_velocity = jnp.dot(
        final_in.reshape(share_rows, feat_width), final_weight, preferred_element_type=jnp.float32
    ).reshape(tokens_out, requests, -1)
    guide_side = lax.axis_index("cfg")
    guided_count = latent.shape[1]
    kept_rows = lax.dynamic_slice_in_dim(own_velocity, guide_side * guided_count, guided_count, 1)
    sent_rows = lax.dynamic_slice_in_dim(
        own_velocity, (1 - guide_side) * guided_count, guided_count, 1
    )
    partner_velocity = from_partner(sent_rows, "cfg", 0)
    is_first = guide_side == 0
    conditional = jnp.where(is_first, kept_rows, partner_velocity)
    unconditional = jnp.where(is_first, partner_velocity, kept_rows)
    velocity = unconditional + guidance_scale * (conditional - unconditional)
    step_size = sigma_of(timesteps + 1) - sigma_of(timesteps)
    step_here = lax.dynamic_slice_in_dim(step_size, guide_side * guided_count, guided_count, 0)
    next_latent = latent + step_here[None, :, None] * velocity
    return (velocity, next_latent)


def solution(mesh):
    return jax.shard_map(
        body,
        mesh=mesh,
        in_specs=(
            P(("seq", "wgt"), "cfg", None),
            P("cfg", "seq", None, None),
            P("cfg", "seq", None),
            P("cfg", "seq"),
            P(),
            P("cfg", None, None, None),
            P(),
            P(None, "seq", "wgt"),
            P(None, "seq", "wgt"),
            P("wgt", "seq"),
            P("seq", "wgt"),
            P("wgt", "seq"),
            P(),
        ),
        out_specs=(P(("seq", "wgt"), "cfg", None), P(("seq", "wgt"), "cfg", None)),
        check_vma=False,
    )
```

```python
import jax
import jax.numpy as jnp
from jax import lax
from jax.experimental import pallas as pl
from jax.experimental.pallas import tpu as pltpu
from jax.sharding import PartitionSpec as P

STEPS = 28


guidance_scale = 3.5
flow_shift = 3.0
eps_norm = 1e-06
masked_score = -1e30


def from_partner(value, axis, bit):
    mask = 2**bit
    pairs = [(source, source ^ mask) for source in range(lax.axis_size(axis))]
    return lax.ppermute(value, axis, pairs)


def layer_norm(values):
    center = jnp.mean(values, axis=-1, keepdims=True)
    centred = values - center
    spread = jnp.mean(centred * centred, axis=-1, keepdims=True)
    return centred * lax.rsqrt(spread + eps_norm)


def head_norm(values, gain_row):
    power = jnp.mean(values * values, axis=-1, keepdims=True)
    return values * lax.rsqrt(power + eps_norm) * gain_row


def sigma_of(index_row):
    time_left = 1.0 - index_row.astype(jnp.float32) / STEPS
    return flow_shift * time_left / (1.0 + (flow_shift - 1.0) * time_left)


def group_sum(partial, groups):
    swapped = lax.all_to_all(partial, "wgt", 0, 0, tiled=True)
    rows = swapped.shape[0] // groups
    return jnp.sum(swapped.reshape(groups, rows, -1).astype(jnp.float32), axis=0)


def make_attention(heads, head_size, text_at, text_here):
    scale = head_size ** (-0.5)

    def kernel(q_ref, kv_ref, mask_ref, o_ref):
        requests, tokens, cols = q_ref.shape
        blocks = kv_ref.shape[0]
        lane = lax.broadcasted_iota(jnp.int32, (1, cols), 1)
        k_txt = kv_ref[:, text_at : text_at + text_here, :].reshape(blocks * text_here, cols)
        v_txt = kv_ref[:, text_at + text_here : text_at + 2 * text_here, :].reshape(
            blocks * text_here, cols
        )
        dims = (((1,), (1,)), ((), ()))
        for r in range(requests):
            q = q_ref[r].astype(jnp.float32)
            k_img = kv_ref[:, 2 * tokens * r : 2 * tokens * r + tokens, :].reshape(
                blocks * tokens, cols
            )
            v_img = kv_ref[:, 2 * tokens * r + tokens : 2 * tokens * (r + 1), :].reshape(
                blocks * tokens, cols
            )
            allowed = mask_ref[r : r + 1, :] > 0.5
            out = jnp.zeros((tokens, cols), jnp.float32)
            for h in range(heads):
                in_head = (lane >= h * head_size) & (lane < (h + 1) * head_size)
                qh = jnp.where(in_head, q, 0.0).astype(jnp.bfloat16)
                s_img = lax.dot_general(qh, k_img, dims, preferred_element_type=jnp.float32) * scale
                s_txt = lax.dot_general(qh, k_txt, dims, preferred_element_type=jnp.float32) * scale
                s_txt = jnp.where(allowed, s_txt, masked_score)
                top = jnp.maximum(
                    jnp.max(s_img, axis=1, keepdims=True), jnp.max(s_txt, axis=1, keepdims=True)
                )
                p_img = jnp.exp(s_img - top)
                p_txt = jnp.exp(s_txt - top)
                total = jnp.sum(p_img, axis=1, keepdims=True) + jnp.sum(p_txt, axis=1, keepdims=True)
                acc = jnp.dot(
                    p_img.astype(jnp.bfloat16), v_img, preferred_element_type=jnp.float32
                ) + jnp.dot(p_txt.astype(jnp.bfloat16), v_txt, preferred_element_type=jnp.float32)
                out = jnp.where(in_head, acc / total, out)
            o_ref[r] = out.astype(o_ref.dtype)

    def run(q, kv, mask):
        return pl.pallas_call(
            kernel,
            out_shape=jax.ShapeDtypeStruct(q.shape, jnp.bfloat16),
            in_specs=[pl.BlockSpec(memory_space=pltpu.VMEM)] * 3,
            out_specs=pl.BlockSpec(memory_space=pltpu.VMEM),
        )(q, kv, mask)

    return run


def mlp_kernel(x_ref, w_ref, o_ref):
    blocks, _, rows, units = w_ref.shape
    expand = w_ref[:, 0].reshape(blocks * rows, units)
    grown = jnp.dot(x_ref[...], expand, preferred_element_type=jnp.float32)
    grown = jax.nn.gelu(grown, approximate=True).astype(jnp.bfloat16)
    contract = w_ref[:, 1].reshape(blocks * rows, units)
    o_ref[...] = lax.dot_general(
        grown, contract, (((1,), (1,)), ((), ())), preferred_element_type=jnp.float32
    ).astype(o_ref.dtype)


def run_mlp(rows_in, weights):
    blocks, _, rows, _ = weights.shape
    return pl.pallas_call(
        mlp_kernel,
        out_shape=jax.ShapeDtypeStruct((rows_in.shape[0], blocks * rows), jnp.bfloat16),
        in_specs=[pl.BlockSpec(memory_space=pltpu.VMEM)] * 2,
        out_specs=pl.BlockSpec(memory_space=pltpu.VMEM),
    )(rows_in, weights)


def body(
    latent,
    img_hidden,
    txt_hidden,
    segments,
    timesteps,
    modulation,
    qk_gain,
    qkv_weight,
    text_weight,
    out_weight,
    expand_weight,
    contract_weight,
    final_weight,
):
    tokens_here = img_hidden.shape[1]
    requests = img_hidden.shape[2]
    feat_width = img_hidden.shape[3]
    head_size = qk_gain.shape[1]
    local_cols = qkv_weight.shape[2]
    heads_here = local_cols // head_size
    text_here = txt_hidden.shape[1]
    seq_size = lax.axis_size("seq")
    wgt_size = lax.axis_size("wgt")
    modulate = modulation[0]
    hidden = img_hidden[0].astype(jnp.float32)
    image_normed = (layer_norm(hidden) * (1.0 + modulate[:, 1]) + modulate[:, 0]).astype(
        jnp.bfloat16
    )
    row_count = tokens_here * requests
    token_rows = image_normed.reshape(row_count, feat_width)
    segment_row = segments[0]
    one_hot = (segment_row[:, None] == jnp.arange(requests, dtype=jnp.int32)[None, :]).astype(
        jnp.float32
    )
    text_mod = jnp.einsum("tr,rkd->tkd", one_hot, modulate[:, 3:5], precision=lax.Precision.HIGHEST)
    text_normed = (
        layer_norm(txt_hidden[0].astype(jnp.float32)) * (1.0 + text_mod[:, 1]) + text_mod[:, 0]
    ).astype(jnp.bfloat16)
    block_rows = qkv_weight.shape[1]
    padded_rows = block_rows + (-block_rows) % 8
    kinds = qkv_weight.shape[0] + text_weight.shape[0]
    all_weights = jnp.transpose(
        jnp.concatenate([qkv_weight[1:], text_weight, qkv_weight[:1]], axis=0), (1, 0, 2)
    ).reshape(block_rows, kinds * local_cols)
    all_weights = jnp.pad(all_weights, ((0, padded_rows - block_rows), (0, 0)))
    piece = lax.all_gather(all_weights, "seq", axis=0, tiled=False)
    mlp_local = jnp.pad(
        jnp.stack([expand_weight, contract_weight.T], axis=0),
        ((0, 0), (0, padded_rows - block_rows), (0, 0)),
    )
    mlp_full = lax.all_gather(mlp_local, "seq", axis=0, tiled=False)
    out_full = lax.all_gather(out_weight, "seq", axis=1, tiled=True)
    both_rows = jnp.concatenate([token_rows, text_normed], axis=0)
    both_count = both_rows.shape[0]
    both_cols = jnp.pad(
        both_rows.T.reshape(seq_size, block_rows, both_count),
        ((0, 0), (0, padded_rows - block_rows), (0, 0)),
    )
    split = (kinds - 1) * local_cols
    kv_term = jnp.einsum(
        "sdr,sdn->rn", both_cols, piece[:, :, :split], preferred_element_type=jnp.float32
    )
    q_term = jnp.einsum(
        "sdr,sdn->rn", both_cols, piece[:, :, split:], preferred_element_type=jnp.float32
    )
    both_term = jnp.concatenate([q_term, kv_term], axis=1).reshape(both_count, kinds, local_cols)
    image_term = both_term[:row_count]
    text_term = both_term[row_count:]
    queries = head_norm(
        image_term[:, 0].reshape(tokens_here, requests, heads_here, head_size), qk_gain[0]
    ).astype(jnp.bfloat16)
    keys_img = head_norm(
        image_term[:, 1].reshape(tokens_here, requests, heads_here, head_size), qk_gain[1]
    ).astype(jnp.bfloat16)
    values_img = image_term[:, 2].reshape(tokens_here, requests, local_cols).astype(jnp.bfloat16)
    keys_txt = head_norm(
        text_term[:, 3].reshape(text_here, heads_here, head_size), qk_gain[1]
    ).astype(jnp.bfloat16)
    values_txt = text_term[:, 4].astype(jnp.bfloat16)
    image_pair = jnp.transpose(
        jnp.stack([keys_img.reshape(tokens_here, requests, local_cols), values_img], axis=0),
        (2, 0, 1, 3),
    ).reshape(requests * 2 * tokens_here, local_cols)
    text_pair = jnp.stack([keys_txt.reshape(text_here, local_cols), values_txt], axis=0).reshape(
        2 * text_here, local_cols
    )
    lanes = local_cols + (-local_cols) % 128
    image_pair = jnp.pad(image_pair, ((0, 0), (0, lanes - local_cols)))
    text_pair = jnp.pad(text_pair, ((0, 0), (0, lanes - local_cols)))
    owner_row = jnp.pad(
        segment_row.astype(jnp.float32).astype(jnp.bfloat16), (0, lanes - text_here)
    )[None, :]
    image_len = requests * 2 * tokens_here
    owner_at = image_len + 2 * text_here
    pad_rows = (-(owner_at + 1)) % 16
    shared = jnp.concatenate(
        [image_pair, text_pair, owner_row, jnp.zeros((pad_rows, lanes), jnp.bfloat16)], axis=0
    )
    shared_piece = lax.all_gather(shared, "seq", axis=0, tiled=False)
    owner_piece = shared_piece[:, owner_at, :text_here].reshape(-1)
    request_ids = jnp.arange(requests, dtype=jnp.float32)
    text_mask = (owner_piece.astype(jnp.float32)[None, :] == request_ids[:, None]).astype(
        jnp.float32
    )
    query_block = jnp.pad(
        jnp.transpose(queries.reshape(tokens_here, requests, local_cols), (1, 0, 2)),
        ((0, 0), (0, 0), (0, lanes - local_cols)),
    )
    attend = make_attention(heads_here, head_size, image_len, text_here)
    attended = attend(query_block, shared_piece, text_mask)
    attended = jnp.transpose(attended[:, :, :local_cols], (1, 0, 2)).reshape(row_count, local_cols)
    share_rows = row_count // wgt_size
    mixed = group_sum(
        jnp.dot(attended, out_full, preferred_element_type=jnp.float32).astype(jnp.bfloat16),
        wgt_size,
    )
    tokens_out = share_rows // requests
    row_place = lax.axis_index("wgt") * share_rows
    base_rows = lax.dynamic_slice_in_dim(
        hidden.reshape(row_count, feat_width), row_place, share_rows, 0
    )
    residual = base_rows.reshape(tokens_out, requests, feat_width) + modulate[:, 2] * mixed.reshape(
        tokens_out, requests, feat_width
    )
    branch_in = (layer_norm(residual) * (1.0 + modulate[:, 6]) + modulate[:, 5]).astype(
        jnp.bfloat16
    )
    branch_rows = lax.all_to_all(
        jnp.broadcast_to(
            branch_in.reshape(1, share_rows, feat_width), (wgt_size, share_rows, feat_width)
        ),
        "wgt",
        0,
        0,
        tiled=True,
    ).reshape(row_count, feat_width)
    padded_rows_in = jnp.pad(
        branch_rows.reshape(row_count, seq_size, block_rows),
        ((0, 0), (0, 0), (0, padded_rows - block_rows)),
    )
    contracted = run_mlp(padded_rows_in.reshape(row_count, seq_size * padded_rows), mlp_full)
    branch = group_sum(contracted, wgt_size)
    branch = branch.reshape(share_rows, seq_size, padded_rows)[:, :, :block_rows].reshape(
        share_rows, feat_width
    )
    second = residual + modulate[:, 7] * branch.reshape(tokens_out, requests, feat_width)
    final_in = (layer_norm(second) * (1.0 + modulate[:, 9]) + modulate[:, 8]).astype(jnp.bfloat16)
    own_velocity = jnp.dot(
        final_in.reshape(share_rows, feat_width), final_weight, preferred_element_type=jnp.float32
    ).reshape(tokens_out, requests, -1)
    guide_side = lax.axis_index("cfg")
    guided_count = latent.shape[1]
    kept_rows = lax.dynamic_slice_in_dim(own_velocity, guide_side * guided_count, guided_count, 1)
    sent_rows = lax.dynamic_slice_in_dim(
        own_velocity, (1 - guide_side) * guided_count, guided_count, 1
    )
    partner_velocity = from_partner(sent_rows, "cfg", 0)
    is_first = guide_side == 0
    conditional = jnp.where(is_first, kept_rows, partner_velocity)
    unconditional = jnp.where(is_first, partner_velocity, kept_rows)
    velocity = unconditional + guidance_scale * (conditional - unconditional)
    step_size = sigma_of(timesteps + 1) - sigma_of(timesteps)
    step_here = lax.dynamic_slice_in_dim(step_size, guide_side * guided_count, guided_count, 0)
    next_latent = latent + step_here[None, :, None] * velocity
    return (velocity, next_latent)


def solution(mesh):
    return jax.shard_map(
        body,
        mesh=mesh,
        in_specs=(
            P(("seq", "wgt"), "cfg", None),
            P("cfg", "seq", None, None),
            P("cfg", "seq", None),
            P("cfg", "seq"),
            P(),
            P("cfg", None, None, None),
            P(),
            P(None, "seq", "wgt"),
            P(None, "seq", "wgt"),
            P("wgt", "seq"),
            P("seq", "wgt"),
            P("wgt", "seq"),
            P(),
        ),
        out_specs=(P(("seq", "wgt"), "cfg", None), P(("seq", "wgt"), "cfg", None)),
        check_vma=False,
    )
```
